256 devices in a mesh: group: 8 (over x, core), dev: 32 (over y, z).
Axes of the slice: x: 4, y: 4, z: 8, core: 2. Of those that a mesh axis runs over, the one named last changes fastest.
Arguments:
- right_side: float32 [5, 512, 2048], P(None, ('group', 'dev')), may hold values from -64 to 64
- jacobi_inverse: float32 [5, 5, 512, 2048], P(None, None, ('group', 'dev')), may hold values from -0.5 to 2.1, as said below
- block_couplings: float32 [4, 5, 5, 512, 2048], P(None, None, None, ('group', 'dev')), may hold values from -0.625 to 0.625
- overset_weight: float32 [8192, 128], P(('group', 'dev')), may hold values from 0.05 to 0.25
- donor_cells: int32 [8192, 128], P(('group', 'dev')), may hold values from 0 to 4095
- receptor_cells: int32 [8192, 128], P(('group', 'dev')), may hold values from 0 to 4095
- aggregate_map: int32 [512, 2048], P(('group', 'dev')), may hold values from 0 to 127
- coarse_inverse: float32 [5, 5, 32768], P(None, None, ('group', 'dev')), may hold values from -0.2 to 0.8, as said below
- coarse_couplings: float32 [2, 5, 5, 32768], P(None, None, None, ('group', 'dev')), may hold values from -1.75 to 1.75
Outputs:
- update: float32 [5, 512, 2048], P(None, ('group', 'dev'))
- new_residual: float32 [5, 512, 2048], P(None, ('group', 'dev'))
The draws below stay inside these ranges and needn't reach their ends.
Inputs may be any that keep to these rules, and one draw needn't show every extreme that they name: `donor_cells`: cell numbers within one block of 4096 cells. `receptor_cells`: cell numbers within one block of 4096 cells. `aggregate_map`: aggregate numbers within one block. `jacobi_inverse`: each 5x5 block has positive diagonal entries. `coarse_inverse`: each 5x5 block has positive diagonal entries.
All inputs are finite; a program needn't handle non-finite values.
Results may differ from the reference program's by a relative error of at most 0.0003.
Values sent between devices are 32-bit elements; how exact they have to be, the bound alone decides.
No kernel may reach another device: no remote copies, remote signals or barrier semaphores. Data moves between devices by JAX's collectives and lax.ppermute only.
A program may use at most 64 MiB of HBM per device.

```python
import math
import jax
import jax.numpy as jnp
from jax import lax

NB = 5
STEPS = 8
SWEEPS = 4
LAYERS = 2
PLANE = 2048
SLOTS = 128
AGG_DEV = 128
CELLS = 4096
NLAYERS = 512
NAGG = 32768
N_DEV = 32
DEVICES = 256


def draw_right_side(key, part):
    base_key = jax.random.fold_in(key, 101)
    key_one, key_two = jax.random.split(base_key, 2)
    full_shape = (NB, NLAYERS, PLANE)
    layer_pos = jnp.arange(NLAYERS, dtype=jnp.float32)[None, :, None] / (NLAYERS - 1)
    rising = jnp.exp(math.log(3.0) * layer_pos)
    roughness = jnp.exp(jax.random.uniform(key_two, full_shape, jnp.float32, 0.0, math.log(10.0))) / 3.0
    noise_vals = jnp.clip(jax.random.normal(key_one, full_shape, jnp.float32), -4.0, 4.0)
    return noise_vals * roughness * rising


def draw_jacobi_inverse(key, part):
    base_key = jax.random.fold_in(key, 202)
    key_one, key_two = jax.random.split(base_key)
    full_shape = (NB, NB, NLAYERS, PLANE)
    identity = jnp.eye(NB, dtype=jnp.float32)[:, :, None, None]
    diagonal = jnp.exp(jax.random.uniform(key_one, (1, NB, NLAYERS, PLANE), jnp.float32, math.log(0.6), math.log(1.6)))
    spread_vals = 0.12 * jnp.clip(jax.random.normal(key_two, full_shape, jnp.float32), -4.0, 4.0)
    return identity * diagonal + spread_vals


def draw_coarse_inverse(key, part):
    base_key = jax.random.fold_in(key, 303)
    key_one, key_two = jax.random.split(base_key)
    full_shape = (NB, NB, NAGG)
    identity = jnp.eye(NB, dtype=jnp.float32)[:, :, None]
    diagonal = jnp.exp(jax.random.uniform(key_one, (1, NB, NAGG), jnp.float32, math.log(0.3), math.log(0.6)))
    spread_vals = 0.05 * jnp.clip(jax.random.normal(key_two, full_shape, jnp.float32), -4.0, 4.0)
    return identity * diagonal + spread_vals


def set_ends(values, rng, low, top_value):
    longest = values.shape.index(max(values.shape))
    spots = []
    for shift in (0, 1):
        where = [jax.random.randint(jax.random.fold_in(rng, axis), (), 0, length) for axis, length in enumerate(values.shape)]
        where[longest] = (where[longest] + shift) % values.shape[longest]
        spots.append(tuple(where))
    return values.at[spots[0]].set(low).at[spots[1]].set(top_value)


def level_of(rng, shape, pieces, least, top_value):
    loudness, own = 1.0, jax.random.fold_in(rng, 6)
    for dim, shards_of in pieces:
        steps = jnp.exp(jax.random.uniform(jax.random.fold_in(own, dim), (shards_of,), jnp.float32, least / len(pieces), top_value / len(pieces)))
        loudness = loudness * jnp.repeat(steps, shape[dim] // shards_of).reshape([-1 if axis == dim else 1 for axis in range(len(shape))])
    return loudness


def scatter_about(key, shape, spread, reach, cuts=(), kind=jnp.bfloat16):
    values = spread * jax.random.normal(key, shape, jnp.float32)
    if cuts:
        values = values * level_of(key, shape, cuts, -0.22, 0.18)
    return jnp.clip(values, -reach, reach).astype(kind)


def setup_inputs(seed: int = 0) -> dict:
    key_list = jax.random.split(jax.random.key(seed), 10)
    return {
        "right_side": draw_right_side(jax.random.fold_in(key_list[9], 71), 0),
        "jacobi_inverse": draw_jacobi_inverse(jax.random.fold_in(key_list[9], 71), 0),
        "block_couplings": scatter_about(key_list[2], (4, NB, NB, NLAYERS, PLANE), 0.1, 0.625, ((3, 256),), jnp.float32),
        "overset_weight": jnp.clip(0.05 + 0.2 * jax.random.uniform(key_list[3], (DEVICES * N_DEV, SLOTS), jnp.float32) ** level_of(key_list[3], (DEVICES * N_DEV, SLOTS), ((0, 256),), -0.2, 0.2), 0.05, 0.25),
        "donor_cells": set_ends(jax.random.randint(key_list[4], (DEVICES * N_DEV, SLOTS), 0, CELLS), jax.random.fold_in(key_list[4], 1), 0, CELLS - 1).astype(jnp.int32),
        "receptor_cells": set_ends(jax.random.randint(key_list[5], (DEVICES * N_DEV, SLOTS), 0, CELLS), jax.random.fold_in(key_list[5], 1), 0, CELLS - 1).astype(jnp.int32),
        "aggregate_map": set_ends(jax.random.randint(key_list[6], (NLAYERS, PLANE), 0, AGG_DEV), jax.random.fold_in(key_list[6], 1), 0, AGG_DEV - 1).astype(jnp.int32),
        "coarse_inverse": draw_coarse_inverse(jax.random.fold_in(key_list[9], 71), 0),
        "coarse_couplings": scatter_about(key_list[8], (2, NB, NB, NAGG), 0.3, 1.75, ((3, 256),), jnp.float32),
    }


BASIS_SCALE = 0.5

def block_apply(blocks, vector):
    return lax.optimization_barrier(jnp.sum(blocks * vector[None], axis=1))

def shift_value(j, count):
    half_index = j // 2
    point = half_index if j % 2 == 0 else count - 1 - half_index
    return 1.0 + 0.5 * math.cos(math.pi * (2 * point + 1) / (2 * count))

def small_solve(gram_matrix):
    count = gram_matrix.shape[0] - 1
    factor = jnp.transpose(jnp.linalg.cholesky(gram_matrix))
    thetas = jnp.array([shift_value(j, count) for j in range(count)], jnp.float32)
    hessenberg = factor[:, :count] * thetas[None, :] + BASIS_SCALE * factor[:, 1:]
    target = factor[:, 0]
    ortho_cols = []
    triangle = {}
    for j in range(count):
        column = hessenberg[:, j]
        for i in range(j):
            factor_ij = jnp.sum(ortho_cols[i] * column)
            triangle[i, j] = factor_ij
            column = column - factor_ij * ortho_cols[i]
        length_val = jnp.sqrt(jnp.sum(column * column))
        triangle[j, j] = length_val
        ortho_cols.append(column / length_val)
    projected = [jnp.sum(q * target) for q in ortho_cols]
    solved = [None] * count
    for j in reversed(range(count)):
        running = projected[j]
        for i in range(j + 1, count):
            running = running - triangle[j, i] * solved[i]
        solved[j] = running / triangle[j, j]
    return (jnp.stack(solved), thetas)

def operate(field, jacobi_inverse, block_couplings, overset_weight, donor_cells, receptor_cells):
    scaled = block_apply(jacobi_inverse, field)
    zero_layer = jnp.zeros_like(scaled[:, :1])
    below_vals = jnp.concatenate([zero_layer, scaled[:, :-1]], axis=1)
    above_vals = jnp.concatenate([scaled[:, 1:], zero_layer], axis=1)
    result = field + block_apply(block_couplings[0], jnp.roll(scaled, 1, axis=2))
    result = result + block_apply(block_couplings[1], jnp.roll(scaled, -1, axis=2))
    result = result + block_apply(block_couplings[2], below_vals)
    result = result + block_apply(block_couplings[3], above_vals)
    source_index = jnp.arange(DEVICES, dtype=jnp.int32)[:, None, None]
    peer_index = jnp.arange(N_DEV, dtype=jnp.int32)[None, :, None]
    donors = donor_cells.reshape(DEVICES, N_DEV, SLOTS)
    source_cell = source_index * CELLS + donors
    target_block = source_index // N_DEV * N_DEV + peer_index
    target_row = (target_block * N_DEV + source_index % N_DEV)[:, :, 0]
    target_cell = target_block * CELLS + receptor_cells[target_row]
    slot_weights = overset_weight[target_row]
    flat_vals = scaled.reshape(NB, -1)
    moved_vals = flat_vals[:, source_cell]
    flat_result = result.reshape(NB, -1).at[:, target_cell].add(-slot_weights[None] * moved_vals)
    return flat_result.reshape(result.shape)

def reference(right_side, jacobi_inverse, block_couplings, overset_weight, donor_cells, receptor_cells, aggregate_map, coarse_inverse, coarse_couplings):
    krylov = [right_side]
    for j in range(STEPS):
        applied = operate(krylov[j], jacobi_inverse, block_couplings, overset_weight, donor_cells, receptor_cells)
        krylov.append((applied - shift_value(j, STEPS) * krylov[j]) / BASIS_SCALE)
    stacked = jnp.stack(krylov)
    gram_matrix = jnp.einsum('iabc,jabc->ij', stacked, stacked, precision=lax.Precision.HIGHEST)
    coeffs, thetas = small_solve(gram_matrix)
    combined = jnp.einsum('i,iabc->abc', coeffs, stacked[:STEPS], precision=lax.Precision.HIGHEST)
    krylov_update = block_apply(jacobi_inverse, combined)
    new_residual = right_side - operate(combined, jacobi_inverse, block_couplings, overset_weight, donor_cells, receptor_cells)
    global_agg = (jnp.arange(NLAYERS, dtype=jnp.int32) // LAYERS)[:, None] * AGG_DEV + aggregate_map
    flat_res = new_residual.reshape(NB, -1)
    coarse_rhs = jax.ops.segment_sum(flat_res.T, global_agg.reshape(-1), num_segments=NAGG).T
    coarse_vals = block_apply(coarse_inverse, coarse_rhs)
    for k in range(SWEEPS - 1):
        zero_col = jnp.zeros_like(coarse_vals[:, :1])
        left_vals = jnp.concatenate([zero_col, coarse_vals[:, :-1]], axis=1)
        right_vals = jnp.concatenate([coarse_vals[:, 1:], zero_col], axis=1)
        coarse_vals = block_apply(coarse_inverse, coarse_rhs - block_apply(coarse_couplings[0], left_vals) - block_apply(coarse_couplings[1], right_vals))
    update = krylov_update + coarse_vals[:, global_agg]
    return (update, new_residual)
```

```python
import math

import jax
import jax.numpy as jnp
from jax import lax
from jax.sharding import PartitionSpec as P

STEPS = 8
SWEEPS = 4


BASIS_SCALE = 0.5


def with_halo(cells, sides, width):
    for axis, dim in sides:
        count = lax.axis_size(axis)
        ends = count - 1
        head = lax.slice_in_dim(cells, 0, width, axis=dim)
        tail = lax.slice_in_dim(cells, cells.shape[dim] - width, cells.shape[dim], axis=dim)
        cells = jnp.concatenate(
            [
                lax.ppermute(tail, axis, [(i, (i + 1) % count) for i in range(ends)]),
                cells,
                lax.ppermute(head, axis, [((i + 1) % count, i) for i in range(ends)]),
            ],
            axis=dim,
        )
    return cells


def block_apply(blocks, vector):
    return jnp.sum(blocks * vector[None], axis=1)


def shift_value(j, count):
    half_index = j // 2
    point = half_index if j % 2 == 0 else count - 1 - half_index
    return 1.0 + 0.5 * math.cos(math.pi * (2 * point + 1) / (2 * count))


def small_solve(gram_matrix):
    count = gram_matrix.shape[0] - 1
    factor = jnp.transpose(jnp.linalg.cholesky(gram_matrix))
    thetas = jnp.array([shift_value(j, count) for j in range(count)], jnp.float32)
    hessenberg = factor[:, :count] * thetas[None, :] + BASIS_SCALE * factor[:, 1:]
    target = factor[:, 0]
    ortho_cols = []
    triangle = {}
    for j in range(count):
        column = hessenberg[:, j]
        for i in range(j):
            factor_ij = jnp.sum(ortho_cols[i] * column)
            triangle[i, j] = factor_ij
            column = column - factor_ij * ortho_cols[i]
        length_val = jnp.sqrt(jnp.sum(column * column))
        triangle[j, j] = length_val
        ortho_cols.append(column / length_val)
    projected = [jnp.sum(q * target) for q in ortho_cols]
    solved = [None] * count
    for j in reversed(range(count)):
        running = projected[j]
        for i in range(j + 1, count):
            running = running - triangle[j, i] * solved[i]
        solved[j] = running / triangle[j, j]
    return (jnp.stack(solved), thetas)


SPLIT = 64


def overset_masks(donor_cells, receptor_cells, overset_weight):
    digits = jnp.arange(SPLIT, dtype=jnp.int32)[:, None]
    donors = donor_cells.reshape(1, -1)
    receptors = receptor_cells.reshape(1, -1)
    weights = overset_weight.reshape(1, -1)
    donor_hi = (donors // SPLIT == digits).astype(jnp.float32)
    donor_lo = (donors % SPLIT == digits).astype(jnp.float32)
    receptor_hi = (receptors // SPLIT == digits).astype(jnp.float32)
    receptor_lo = jnp.where(receptors % SPLIT == digits, weights, 0.0)
    return donor_hi, donor_lo, receptor_hi, receptor_lo


def operate(field, jacobi_inverse, block_couplings, masks):
    donor_hi, donor_lo, receptor_hi, receptor_lo = masks
    scaled = block_apply(jacobi_inverse, field)
    padded = with_halo(scaled, ((("group", "dev"), 1),), 1)
    result = field + block_apply(block_couplings[0], jnp.roll(scaled, 1, axis=2))
    result = result + block_apply(block_couplings[1], jnp.roll(scaled, -1, axis=2))
    result = result + block_apply(block_couplings[2], padded[:, :-2])
    result = result + block_apply(block_couplings[3], padded[:, 2:])
    comps = scaled.shape[0]
    split_vals = scaled.reshape(comps, -1, SPLIT)
    partial = jnp.einsum("chl,hs->cls", split_vals, donor_hi, precision=lax.Precision.HIGHEST)
    outgoing = jnp.sum(partial * donor_lo[None], axis=1)
    outgoing = outgoing.reshape(comps, lax.axis_size("dev"), -1)
    incoming = lax.all_to_all(outgoing, "dev", split_axis=1, concat_axis=1, tiled=True)
    incoming = incoming.reshape(comps, 1, -1)
    spread = incoming * receptor_lo[None]
    moved = jnp.einsum("hs,cls->chl", receptor_hi, spread, precision=lax.Precision.HIGHEST)
    return result - moved.reshape(result.shape)


def layer_onehot(labels, count):
    return (labels[:, None] == jnp.arange(count, dtype=jnp.int32)[None, :]).astype(jnp.float32)


def restrict_field(field, aggregate_map, count):
    totals = jnp.zeros((field.shape[0], count), jnp.float32)
    for k in range(field.shape[1]):
        totals = totals + jnp.dot(
            field[:, k], layer_onehot(aggregate_map[k], count), precision=lax.Precision.HIGHEST
        )
    return totals


def prolong_field(coarse_vals, aggregate_map):
    count = coarse_vals.shape[1]
    layers_out = [
        jnp.dot(
            coarse_vals,
            jnp.transpose(layer_onehot(aggregate_map[k], count)),
            precision=lax.Precision.HIGHEST,
        )
        for k in range(aggregate_map.shape[0])
    ]
    return jnp.stack(layers_out, axis=1)


def body(
    right_side,
    jacobi_inverse,
    block_couplings,
    overset_weight,
    donor_cells,
    receptor_cells,
    aggregate_map,
    coarse_inverse,
    coarse_couplings,
):
    masks = overset_masks(donor_cells, receptor_cells, overset_weight)
    krylov = [right_side]
    for j in range(STEPS):
        applied = operate(krylov[j], jacobi_inverse, block_couplings, masks)
        krylov.append((applied - shift_value(j, STEPS) * krylov[j]) / BASIS_SCALE)
    stacked = jnp.stack(krylov)
    local_gram = jnp.einsum("iabc,jabc->ij", stacked, stacked, precision=lax.Precision.HIGHEST)
    gram_total = lax.psum(local_gram, ("group", "dev"))
    coeffs, thetas = small_solve(gram_total)
    combined = jnp.einsum("i,iabc->abc", coeffs, stacked[:STEPS], precision=lax.Precision.HIGHEST)
    krylov_update = block_apply(jacobi_inverse, combined)
    new_residual = right_side - operate(combined, jacobi_inverse, block_couplings, masks)
    agg_count = coarse_inverse.shape[2]
    local_rhs = restrict_field(new_residual, aggregate_map, agg_count)
    own_vals = block_apply(coarse_inverse, local_rhs)
    for k in range(SWEEPS - 1):
        padded = with_halo(own_vals, ((("group", "dev"), 1),), 1)
        own_vals = block_apply(
            coarse_inverse,
            local_rhs
            - block_apply(coarse_couplings[0], padded[:, :-2])
            - block_apply(coarse_couplings[1], padded[:, 2:]),
        )
    update = krylov_update + prolong_field(own_vals, aggregate_map)
    return (update, new_residual)


def solution(mesh):
    return jax.shard_map(
        body,
        mesh=mesh,
        in_specs=(
            P(None, ("group", "dev"), None),
            P(None, None, ("group", "dev"), None),
            P(None, None, None, ("group", "dev"), None),
            P(("group", "dev"), None),
            P(("group", "dev"), None),
            P(("group", "dev"), None),
            P(("group", "dev"), None),
            P(None, None, ("group", "dev")),
            P(None, None, None, ("group", "dev")),
        ),
        out_specs=(P(None, ("group", "dev"), None), P(None, ("group", "dev"), None)),
        check_vma=False,
    )
```

```python
import math

import jax
import jax.numpy as jnp
from jax import lax
from jax.sharding import PartitionSpec as P

STEPS = 8
SWEEPS = 4


BASIS_SCALE = 0.5


def with_halo(cells, sides, width):
    for axis, dim in sides:
        count = lax.axis_size(axis)
        ends = count - 1
        head = lax.slice_in_dim(cells, 0, width, axis=dim)
        tail = lax.slice_in_dim(cells, cells.shape[dim] - width, cells.shape[dim], axis=dim)
        cells = jnp.concatenate(
            [
                lax.ppermute(tail, axis, [(i, (i + 1) % count) for i in range(ends)]),
                cells,
                lax.ppermute(head, axis, [((i + 1) % count, i) for i in range(ends)]),
            ],
            axis=dim,
        )
    return cells


def block_apply(blocks, vector):
    return jnp.sum(blocks * vector[None], axis=1)


def shift_value(j, count):
    half_index = j // 2
    point = half_index if j % 2 == 0 else count - 1 - half_index
    return 1.0 + 0.5 * math.cos(math.pi * (2 * point + 1) / (2 * count))


def small_solve(gram_matrix):
    count = gram_matrix.shape[0] - 1
    factor = jnp.transpose(jnp.linalg.cholesky(gram_matrix))
    thetas = jnp.array([shift_value(j, count) for j in range(count)], jnp.float32)
    hessenberg = factor[:, :count] * thetas[None, :] + BASIS_SCALE * factor[:, 1:]
    target = factor[:, 0]
    ortho_cols = []
    triangle = {}
    for j in range(count):
        column = hessenberg[:, j]
        for i in range(j):
            factor_ij = jnp.sum(ortho_cols[i] * column)
            triangle[i, j] = factor_ij
            column = column - factor_ij * ortho_cols[i]
        length_val = jnp.sqrt(jnp.sum(column * column))
        triangle[j, j] = length_val
        ortho_cols.append(column / length_val)
    projected = [jnp.sum(q * target) for q in ortho_cols]
    solved = [None] * count
    for j in reversed(range(count)):
        running = projected[j]
        for i in range(j + 1, count):
            running = running - triangle[j, i] * solved[i]
        solved[j] = running / triangle[j, j]
    return (jnp.stack(solved), thetas)


SPLIT = 64


def overset_masks(donor_cells, receptor_cells, overset_weight):
    digits = jnp.arange(SPLIT, dtype=jnp.int32)[:, None]
    donors = donor_cells.reshape(1, -1)
    receptors = receptor_cells.reshape(1, -1)
    weights = overset_weight.reshape(1, -1)
    donor_hi = (donors // SPLIT == digits).astype(jnp.float32)
    donor_lo = (donors % SPLIT == digits).astype(jnp.float32)
    receptor_hi = (receptors // SPLIT == digits).astype(jnp.float32)
    receptor_lo = jnp.where(receptors % SPLIT == digits, weights, 0.0)
    return donor_hi, donor_lo, receptor_hi, receptor_lo


def operate(field, jacobi_inverse, block_couplings, masks):
    donor_hi, donor_lo, receptor_hi, receptor_lo = masks
    scaled = block_apply(jacobi_inverse, field)
    padded = with_halo(scaled, ((("group", "dev"), 1),), 1)
    result = field + block_apply(block_couplings[0], jnp.roll(scaled, 1, axis=2))
    result = result + block_apply(block_couplings[1], jnp.roll(scaled, -1, axis=2))
    result = result + block_apply(block_couplings[2], padded[:, :-2])
    result = result + block_apply(block_couplings[3], padded[:, 2:])
    comps = scaled.shape[0]
    split_vals = scaled.reshape(comps, -1, SPLIT)
    partial = jnp.einsum("chl,hs->cls", split_vals, donor_hi, precision=lax.Precision.HIGHEST)
    outgoing = jnp.sum(partial * donor_lo[None], axis=1)
    outgoing = outgoing.reshape(comps, lax.axis_size("dev"), -1)
    incoming = lax.all_to_all(outgoing, "dev", split_axis=1, concat_axis=1, tiled=True)
    incoming = incoming.reshape(comps, 1, -1)
    spread = incoming * receptor_lo[None]
    moved = jnp.einsum("hs,cls->chl", receptor_hi, spread, precision=lax.Precision.HIGHEST)
    return result - moved.reshape(result.shape)


def layer_onehot(labels, count):
    return (labels[:, None] == jnp.arange(count, dtype=jnp.int32)[None, :]).astype(jnp.float32)


def restrict_field(field, aggregate_map, count):
    totals = jnp.zeros((field.shape[0], count), jnp.float32)
    for k in range(field.shape[1]):
        totals = totals + jnp.dot(
            field[:, k], layer_onehot(aggregate_map[k], count), precision=lax.Precision.HIGHEST
        )
    return totals


def prolong_field(coarse_vals, aggregate_map):
    count = coarse_vals.shape[1]
    layers_out = [
        jnp.dot(
            coarse_vals,
            jnp.transpose(layer_onehot(aggregate_map[k], count)),
            precision=lax.Precision.HIGHEST,
        )
        for k in range(aggregate_map.shape[0])
    ]
    return jnp.stack(layers_out, axis=1)


def body(
    right_side,
    jacobi_inverse,
    block_couplings,
    overset_weight,
    donor_cells,
    receptor_cells,
    aggregate_map,
    coarse_inverse,
    coarse_couplings,
):
    masks = overset_masks(donor_cells, receptor_cells, overset_weight)
    krylov = [right_side]
    for j in range(STEPS):
        applied = operate(krylov[j], jacobi_inverse, block_couplings, masks)
        krylov.append((applied - shift_value(j, STEPS) * krylov[j]) / BASIS_SCALE)
    stacked = jnp.stack(krylov)
    local_gram = jnp.einsum("iabc,jabc->ij", stacked, stacked, precision=lax.Precision.HIGHEST)
    gram_total = lax.psum(local_gram, ("group", "dev"))
    coeffs, thetas = small_solve(gram_total)
    combined = jnp.einsum("i,iabc->abc", coeffs, stacked[:STEPS], precision=lax.Precision.HIGHEST)
    krylov_update = block_apply(jacobi_inverse, combined)
    applied_combined = sum(
        coeffs[j] * (BASIS_SCALE * krylov[j + 1] + thetas[j] * krylov[j]) for j in range(STEPS)
    )
    new_residual = right_side - applied_combined
    agg_count = coarse_inverse.shape[2]
    local_rhs = restrict_field(new_residual, aggregate_map, agg_count)
    own_vals = block_apply(coarse_inverse, local_rhs)
    for k in range(SWEEPS - 1):
        padded = with_halo(own_vals, ((("group", "dev"), 1),), 1)
        own_vals = block_apply(
            coarse_inverse,
            local_rhs
            - block_apply(coarse_couplings[0], padded[:, :-2])
            - block_apply(coarse_couplings[1], padded[:, 2:]),
        )
    update = krylov_update + prolong_field(own_vals, aggregate_map)
    return (update, new_residual)


def solution(mesh):
    return jax.shard_map(
        body,
        mesh=mesh,
        in_specs=(
            P(None, ("group", "dev"), None),
            P(None, None, ("group", "dev"), None),
            P(None, None, None, ("group", "dev"), None),
            P(("group", "dev"), None),
            P(("group", "dev"), None),
            P(("group", "dev"), None),
            P(("group", "dev"), None),
            P(None, None, ("group", "dev")),
            P(None, None, None, ("group", "dev")),
        ),
        out_specs=(P(None, ("group", "dev"), None), P(None, ("group", "dev"), None)),
        check_vma=False,
    )
```

```python
import math

import jax
import jax.numpy as jnp
from jax import lax
from jax.sharding import PartitionSpec as P

STEPS = 8
SWEEPS = 4


BASIS_SCALE = 0.5


def with_halo(cells, sides, width):
    for axis, dim in sides:
        count = lax.axis_size(axis)
        ends = count - 1
        head = lax.slice_in_dim(cells, 0, width, axis=dim)
        tail = lax.slice_in_dim(cells, cells.shape[dim] - width, cells.shape[dim], axis=dim)
        cells = jnp.concatenate(
            [
                lax.ppermute(tail, axis, [(i, (i + 1) % count) for i in range(ends)]),
                cells,
                lax.ppermute(head, axis, [((i + 1) % count, i) for i in range(ends)]),
            ],
            axis=dim,
        )
    return cells


def gathered_sum(values, axis):
    count = lax.axis_size(axis)
    copies = jnp.broadcast_to(values[None], (count,) + values.shape)
    return jnp.sum(lax.all_to_all(copies, axis, 0, 0, tiled=True), axis=0)


def block_apply(blocks, vector):
    return jnp.sum(blocks * vector[None], axis=1)


def shift_value(j, count):
    half_index = j // 2
    point = half_index if j % 2 == 0 else count - 1 - half_index
    return 1.0 + 0.5 * math.cos(math.pi * (2 * point + 1) / (2 * count))


def small_solve(gram_matrix):
    count = gram_matrix.shape[0] - 1
    factor = jnp.transpose(jnp.linalg.cholesky(gram_matrix))
    thetas = jnp.array([shift_value(j, count) for j in range(count)], jnp.float32)
    hessenberg = factor[:, :count] * thetas[None, :] + BASIS_SCALE * factor[:, 1:]
    target = factor[:, 0]
    ortho_cols = []
    triangle = {}
    for j in range(count):
        column = hessenberg[:, j]
        for i in range(j):
            factor_ij = jnp.sum(ortho_cols[i] * column)
            triangle[i, j] = factor_ij
            column = column - factor_ij * ortho_cols[i]
        length_val = jnp.sqrt(jnp.sum(column * column))
        triangle[j, j] = length_val
        ortho_cols.append(column / length_val)
    projected = [jnp.sum(q * target) for q in ortho_cols]
    solved = [None] * count
    for j in reversed(range(count)):
        running = projected[j]
        for i in range(j + 1, count):
            running = running - triangle[j, i] * solved[i]
        solved[j] = running / triangle[j, j]
    return (jnp.stack(solved), thetas)


SPLIT = 64


def overset_masks(donor_cells, receptor_cells, overset_weight):
    digits = jnp.arange(SPLIT, dtype=jnp.int32)[:, None]
    donors = donor_cells.reshape(1, -1)
    receptors = receptor_cells.reshape(1, -1)
    weights = overset_weight.reshape(1, -1)
    donor_hi = (donors // SPLIT == digits).astype(jnp.float32)
    donor_lo = (donors % SPLIT == digits).astype(jnp.float32)
    receptor_hi = (receptors // SPLIT == digits).astype(jnp.float32)
    receptor_lo = jnp.where(receptors % SPLIT == digits, weights, 0.0)
    return donor_hi, donor_lo, receptor_hi, receptor_lo


def operate(field, jacobi_inverse, block_couplings, masks):
    donor_hi, donor_lo, receptor_hi, receptor_lo = masks
    scaled = block_apply(jacobi_inverse, field)
    padded = with_halo(scaled, ((("group", "dev"), 1),), 1)
    result = field + block_apply(block_couplings[0], jnp.roll(scaled, 1, axis=2))
    result = result + block_apply(block_couplings[1], jnp.roll(scaled, -1, axis=2))
    result = result + block_apply(block_couplings[2], padded[:, :-2])
    result = result + block_apply(block_couplings[3], padded[:, 2:])
    comps = scaled.shape[0]
    split_vals = scaled.reshape(comps, -1, SPLIT)
    partial = jnp.einsum("chl,hs->cls", split_vals, donor_hi, precision=lax.Precision.HIGHEST)
    outgoing = jnp.sum(partial * donor_lo[None], axis=1)
    outgoing = outgoing.reshape(comps, lax.axis_size("dev"), -1)
    incoming = lax.all_to_all(outgoing, "dev", split_axis=1, concat_axis=1, tiled=True)
    incoming = incoming.reshape(comps, 1, -1)
    spread = incoming * receptor_lo[None]
    moved = jnp.einsum("hs,cls->chl", receptor_hi, spread, precision=lax.Precision.HIGHEST)
    return result - moved.reshape(result.shape)


def layer_onehot(labels, count):
    return (labels[:, None] == jnp.arange(count, dtype=jnp.int32)[None, :]).astype(jnp.float32)


def restrict_field(field, aggregate_map, count):
    totals = jnp.zeros((field.shape[0], count), jnp.float32)
    for k in range(field.shape[1]):
        totals = totals + jnp.dot(
            field[:, k], layer_onehot(aggregate_map[k], count), precision=lax.Precision.HIGHEST
        )
    return totals


def prolong_field(coarse_vals, aggregate_map):
    count = coarse_vals.shape[1]
    layers_out = [
        jnp.dot(
            coarse_vals,
            jnp.transpose(layer_onehot(aggregate_map[k], count)),
            precision=lax.Precision.HIGHEST,
        )
        for k in range(aggregate_map.shape[0])
    ]
    return jnp.stack(layers_out, axis=1)


def body(
    right_side,
    jacobi_inverse,
    block_couplings,
    overset_weight,
    donor_cells,
    receptor_cells,
    aggregate_map,
    coarse_inverse,
    coarse_couplings,
):
    masks = overset_masks(donor_cells, receptor_cells, overset_weight)
    krylov = [right_side]
    for j in range(STEPS):
        applied = operate(krylov[j], jacobi_inverse, block_couplings, masks)
        krylov.append((applied - shift_value(j, STEPS) * krylov[j]) / BASIS_SCALE)
    stacked = jnp.stack(krylov)
    local_gram = jnp.einsum("iabc,jabc->ij", stacked, stacked, precision=lax.Precision.HIGHEST)
    gram_total = gathered_sum(gathered_sum(local_gram, "dev"), "group")
    coeffs, thetas = small_solve(gram_total)
    combined = jnp.einsum("i,iabc->abc", coeffs, stacked[:STEPS], precision=lax.Precision.HIGHEST)
    krylov_update = block_apply(jacobi_inverse, combined)
    applied_combined = sum(
        coeffs[j] * (BASIS_SCALE * krylov[j + 1] + thetas[j] * krylov[j]) for j in range(STEPS)
    )
    new_residual = right_side - applied_combined
    agg_count = coarse_inverse.shape[2]
    local_rhs = restrict_field(new_residual, aggregate_map, agg_count)
    own_vals = block_apply(coarse_inverse, local_rhs)
    for k in range(SWEEPS - 1):
        padded = with_halo(own_vals, ((("group", "dev"), 1),), 1)
        own_vals = block_apply(
            coarse_inverse,
            local_rhs
            - block_apply(coarse_couplings[0], padded[:, :-2])
            - block_apply(coarse_couplings[1], padded[:, 2:]),
        )
    update = krylov_update + prolong_field(own_vals, aggregate_map)
    return (update, new_residual)


def solution(mesh):
    return jax.shard_map(
        body,
        mesh=mesh,
        in_specs=(
            P(None, ("group", "dev"), None),
            P(None, None, ("group", "dev"), None),
            P(None, None, None, ("group", "dev"), None),
            P(("group", "dev"), None),
            P(("group", "dev"), None),
            P(("group", "dev"), None),
            P(("group", "dev"), None),
            P(None, None, ("group", "dev")),
            P(None, None, None, ("group", "dev")),
        ),
        out_specs=(P(None, ("group", "dev"), None), P(None, ("group", "dev"), None)),
        check_vma=False,
    )
```

```python
import math

import jax
import jax.numpy as jnp
from jax import lax
from jax.sharding import PartitionSpec as P

STEPS = 8
SWEEPS = 4


BASIS_SCALE = 0.5


def with_halo(cells, sides, width):
    for axis, dim in sides:
        count = lax.axis_size(axis)
        ends = count - 1
        head = lax.slice_in_dim(cells, 0, width, axis=dim)
        tail = lax.slice_in_dim(cells, cells.shape[dim] - width, cells.shape[dim], axis=dim)
        cells = jnp.concatenate(
            [
                lax.ppermute(tail, axis, [(i, (i + 1) % count) for i in range(ends)]),
                cells,
                lax.ppermute(head, axis, [((i + 1) % count, i) for i in range(ends)]),
            ],
            axis=dim,
        )
    return cells


def gathered_sum(values, axis):
    count = lax.axis_size(axis)
    copies = jnp.broadcast_to(values[None], (count,) + values.shape)
    return jnp.sum(lax.all_to_all(copies, axis, 0, 0, tiled=True), axis=0)


def block_apply(blocks, vector):
    return jnp.sum(blocks * vector[None], axis=1)


def shift_value(j, count):
    half_index = j // 2
    point = half_index if j % 2 == 0 else count - 1 - half_index
    return 1.0 + 0.5 * math.cos(math.pi * (2 * point + 1) / (2 * count))


def small_solve(gram_matrix):
    count = gram_matrix.shape[0] - 1
    factor = jnp.transpose(jnp.linalg.cholesky(gram_matrix))
    thetas = jnp.array([shift_value(j, count) for j in range(count)], jnp.float32)
    hessenberg = factor[:, :count] * thetas[None, :] + BASIS_SCALE * factor[:, 1:]
    target = factor[:, 0]
    ortho_cols = []
    triangle = {}
    for j in range(count):
        column = hessenberg[:, j]
        for i in range(j):
            factor_ij = jnp.sum(ortho_cols[i] * column)
            triangle[i, j] = factor_ij
            column = column - factor_ij * ortho_cols[i]
        length_val = jnp.sqrt(jnp.sum(column * column))
        triangle[j, j] = length_val
        ortho_cols.append(column / length_val)
    projected = [jnp.sum(q * target) for q in ortho_cols]
    solved = [None] * count
    for j in reversed(range(count)):
        running = projected[j]
        for i in range(j + 1, count):
            running = running - triangle[j, i] * solved[i]
        solved[j] = running / triangle[j, j]
    return (jnp.stack(solved), thetas)


LOW = 256
HIGH = 16


def bf16_pieces(values):
    first = lax.reduce_precision(values, exponent_bits=8, mantissa_bits=7)
    rest = values - first
    second = lax.reduce_precision(rest, exponent_bits=8, mantissa_bits=7)
    third = rest - second
    return [piece.astype(jnp.bfloat16) for piece in (first, second, third)]


def overset_masks(donor_cells, receptor_cells, overset_weight):
    low_digits = jnp.arange(LOW, dtype=jnp.int32)[:, None]
    high_digits = jnp.arange(HIGH, dtype=jnp.int32)[:, None]
    donors = donor_cells.reshape(1, -1)
    receptors = receptor_cells.reshape(1, -1)
    weights = overset_weight.reshape(1, -1)
    donor_low = (donors % LOW == low_digits).astype(jnp.bfloat16)
    donor_low = jnp.concatenate([donor_low] * 3, axis=0)
    donor_high = (donors // LOW == high_digits).astype(jnp.float32)
    receptor_low = (receptors % LOW == low_digits).astype(jnp.bfloat16)
    receptor_high = jnp.where(receptors // LOW == high_digits, weights, 0.0)
    return donor_low, donor_high, receptor_low, receptor_high


def operate(field, jacobi_inverse, block_couplings, masks):
    donor_low, donor_high, receptor_low, receptor_high = masks
    scaled = block_apply(jacobi_inverse, field)
    padded = with_halo(scaled, ((("group", "dev"), 1),), 1)
    result = field + block_apply(block_couplings[0], jnp.roll(scaled, 1, axis=2))
    result = result + block_apply(block_couplings[1], jnp.roll(scaled, -1, axis=2))
    result = result + block_apply(block_couplings[2], padded[:, :-2])
    result = result + block_apply(block_couplings[3], padded[:, 2:])
    comps = scaled.shape[0]
    split_vals = scaled.reshape(comps, -1, LOW)
    stacked_pieces = jnp.concatenate(bf16_pieces(split_vals), axis=2)
    partial = jnp.einsum(
        "chl,ls->chs", stacked_pieces, donor_low, preferred_element_type=jnp.float32
    )
    outgoing = jnp.sum(partial * donor_high[None], axis=1)
    outgoing = outgoing.reshape(comps, lax.axis_size("dev"), -1)
    incoming = lax.all_to_all(outgoing, "dev", split_axis=1, concat_axis=1, tiled=True)
    incoming = incoming.reshape(comps, 1, -1)
    spread = incoming * receptor_high[None]
    moved_pieces = [
        jnp.einsum("chs,ls->chl", piece, receptor_low, preferred_element_type=jnp.float32)
        for piece in bf16_pieces(spread)
    ]
    moved = (moved_pieces[0] + moved_pieces[1]) + moved_pieces[2]
    return result - moved.reshape(result.shape)


def layer_onehot(labels, count):
    return (labels[:, None] == jnp.arange(count, dtype=jnp.int32)[None, :]).astype(jnp.float32)


def restrict_field(field, aggregate_map, count):
    totals = jnp.zeros((field.shape[0], count), jnp.float32)
    for k in range(field.shape[1]):
        totals = totals + jnp.dot(
            field[:, k], layer_onehot(aggregate_map[k], count), precision=lax.Precision.HIGHEST
        )
    return totals


def prolong_field(coarse_vals, aggregate_map):
    count = coarse_vals.shape[1]
    layers_out = [
        jnp.dot(
            coarse_vals,
            jnp.transpose(layer_onehot(aggregate_map[k], count)),
            precision=lax.Precision.HIGHEST,
        )
        for k in range(aggregate_map.shape[0])
    ]
    return jnp.stack(layers_out, axis=1)


def body(
    right_side,
    jacobi_inverse,
    block_couplings,
    overset_weight,
    donor_cells,
    receptor_cells,
    aggregate_map,
    coarse_inverse,
    coarse_couplings,
):
    masks = overset_masks(donor_cells, receptor_cells, overset_weight)
    krylov = [right_side]
    for j in range(STEPS):
        applied = operate(krylov[j], jacobi_inverse, block_couplings, masks)
        krylov.append((applied - shift_value(j, STEPS) * krylov[j]) / BASIS_SCALE)
    stacked = jnp.stack(krylov)
    local_gram = jnp.einsum("iabc,jabc->ij", stacked, stacked, precision=lax.Precision.HIGHEST)
    gram_total = gathered_sum(gathered_sum(local_gram, "dev"), "group")
    coeffs, thetas = small_solve(gram_total)
    combined = jnp.einsum("i,iabc->abc", coeffs, stacked[:STEPS], precision=lax.Precision.HIGHEST)
    krylov_update = block_apply(jacobi_inverse, combined)
    applied_combined = sum(
        coeffs[j] * (BASIS_SCALE * krylov[j + 1] + thetas[j] * krylov[j]) for j in range(STEPS)
    )
    new_residual = right_side - applied_combined
    agg_count = coarse_inverse.shape[2]
    local_rhs = restrict_field(new_residual, aggregate_map, agg_count)
    own_vals = block_apply(coarse_inverse, local_rhs)
    for k in range(SWEEPS - 1):
        padded = with_halo(own_vals, ((("group", "dev"), 1),), 1)
        own_vals = block_apply(
            coarse_inverse,
            local_rhs
            - block_apply(coarse_couplings[0], padded[:, :-2])
            - block_apply(coarse_couplings[1], padded[:, 2:]),
        )
    update = krylov_update + prolong_field(own_vals, aggregate_map)
    return (update, new_residual)


def solution(mesh):
    return jax.shard_map(
        body,
        mesh=mesh,
        in_specs=(
            P(None, ("group", "dev"), None),
            P(None, None, ("group", "dev"), None),
            P(None, None, None, ("group", "dev"), None),
            P(("group", "dev"), None),
            P(("group", "dev"), None),
            P(("group", "dev"), None),
            P(("group", "dev"), None),
            P(None, None, ("group", "dev")),
            P(None, None, None, ("group", "dev")),
        ),
        out_specs=(P(None, ("group", "dev"), None), P(None, ("group", "dev"), None)),
        check_vma=False,
    )
```

```python
import math

import jax
import jax.numpy as jnp
from jax import lax
from jax.experimental import pallas as pl
from jax.sharding import PartitionSpec as P

STEPS = 8
SWEEPS = 4


BASIS_SCALE = 0.5


def with_halo(cells, sides, width):
    for axis, dim in sides:
        count = lax.axis_size(axis)
        ends = count - 1
        head = lax.slice_in_dim(cells, 0, width, axis=dim)
        tail = lax.slice_in_dim(cells, cells.shape[dim] - width, cells.shape[dim], axis=dim)
        cells = jnp.concatenate(
            [
                lax.ppermute(tail, axis, [(i, (i + 1) % count) for i in range(ends)]),
                cells,
                lax.ppermute(head, axis, [((i + 1) % count, i) for i in range(ends)]),
            ],
            axis=dim,
        )
    return cells


def gathered_sum(values, axis):
    count = lax.axis_size(axis)
    copies = jnp.broadcast_to(values[None], (count,) + values.shape)
    return jnp.sum(lax.all_to_all(copies, axis, 0, 0, tiled=True), axis=0)


def block_apply(blocks, vector):
    return jnp.sum(blocks * vector[None], axis=1)


def shift_value(j, count):
    half_index = j // 2
    point = half_index if j % 2 == 0 else count - 1 - half_index
    return 1.0 + 0.5 * math.cos(math.pi * (2 * point + 1) / (2 * count))


def least_squares_kernel(hessenberg_ref, target_ref, coeffs_ref):
    hessenberg = hessenberg_ref[...]
    target = target_ref[...]
    count = hessenberg.shape[1]
    ortho_cols = []
    triangle = {}
    for j in range(count):
        column = hessenberg[:, j : j + 1]
        for i in range(j):
            factor_ij = jnp.sum(ortho_cols[i] * column, axis=0, keepdims=True)
            triangle[i, j] = factor_ij
            column = column - factor_ij * ortho_cols[i]
        length_val = jnp.sqrt(jnp.sum(column * column, axis=0, keepdims=True))
        triangle[j, j] = length_val
        ortho_cols.append(column / length_val)
    projected = [jnp.sum(q * target, axis=0, keepdims=True) for q in ortho_cols]
    solved = [None] * count
    for j in reversed(range(count)):
        running = projected[j]
        for i in range(j + 1, count):
            running = running - triangle[j, i] * solved[i]
        solved[j] = running / triangle[j, j]
    lanes = lax.broadcasted_iota(jnp.int32, (1, count), 1)
    coeffs = jnp.zeros((1, count), jnp.float32)
    for j in range(count):
        coeffs = jnp.where(lanes == j, solved[j], coeffs)
    coeffs_ref[...] = coeffs


def small_solve(gram_matrix):
    count = gram_matrix.shape[0] - 1
    factor = jnp.transpose(jnp.linalg.cholesky(gram_matrix))
    thetas = jnp.array([shift_value(j, count) for j in range(count)], jnp.float32)
    hessenberg = factor[:, :count] * thetas[None, :] + BASIS_SCALE * factor[:, 1:]
    target = factor[:, :1]
    coeffs = pl.pallas_call(
        least_squares_kernel,
        out_shape=jax.ShapeDtypeStruct((1, count), jnp.float32),
    )(hessenberg, target)
    return (coeffs[0], thetas)


SPLIT = 64


def overset_masks(donor_cells, receptor_cells, overset_weight):
    digits = jnp.arange(SPLIT, dtype=jnp.int32)[:, None]
    donors = donor_cells.reshape(1, -1)
    receptors = receptor_cells.reshape(1, -1)
    weights = overset_weight.reshape(1, -1)
    donor_hi = (donors // SPLIT == digits).astype(jnp.float32)
    donor_lo = (donors % SPLIT == digits).astype(jnp.float32)
    receptor_hi = (receptors // SPLIT == digits).astype(jnp.float32)
    receptor_lo = jnp.where(receptors % SPLIT == digits, weights, 0.0)
    return donor_hi, donor_lo, receptor_hi, receptor_lo


def operate(field, jacobi_inverse, block_couplings, masks):
    donor_hi, donor_lo, receptor_hi, receptor_lo = masks
    scaled = block_apply(jacobi_inverse, field)
    padded = with_halo(scaled, ((("group", "dev"), 1),), 1)
    result = field + block_apply(block_couplings[0], jnp.roll(scaled, 1, axis=2))
    result = result + block_apply(block_couplings[1], jnp.roll(scaled, -1, axis=2))
    result = result + block_apply(block_couplings[2], padded[:, :-2])
    result = result + block_apply(block_couplings[3], padded[:, 2:])
    comps = scaled.shape[0]
    split_vals = scaled.reshape(comps, -1, SPLIT)
    partial = jnp.einsum("chl,hs->cls", split_vals, donor_hi, precision=lax.Precision.HIGHEST)
    outgoing = jnp.sum(partial * donor_lo[None], axis=1)
    outgoing = outgoing.reshape(comps, lax.axis_size("dev"), -1)
    incoming = lax.all_to_all(outgoing, "dev", split_axis=1, concat_axis=1, tiled=True)
    incoming = incoming.reshape(comps, 1, -1)
    spread = incoming * receptor_lo[None]
    moved = jnp.einsum("hs,cls->chl", receptor_hi, spread, precision=lax.Precision.HIGHEST)
    return result - moved.reshape(result.shape)


def layer_onehot(labels, count):
    return (labels[:, None] == jnp.arange(count, dtype=jnp.int32)[None, :]).astype(jnp.float32)


def restrict_field(field, aggregate_map, count):
    totals = jnp.zeros((field.shape[0], count), jnp.float32)
    for k in range(field.shape[1]):
        totals = totals + jnp.dot(
            field[:, k], layer_onehot(aggregate_map[k], count), precision=lax.Precision.HIGHEST
        )
    return totals


def prolong_field(coarse_vals, aggregate_map):
    count = coarse_vals.shape[1]
    layers_out = [
        jnp.dot(
            coarse_vals,
            jnp.transpose(layer_onehot(aggregate_map[k], count)),
            precision=lax.Precision.HIGHEST,
        )
        for k in range(aggregate_map.shape[0])
    ]
    return jnp.stack(layers_out, axis=1)


def body(
    right_side,
    jacobi_inverse,
    block_couplings,
    overset_weight,
    donor_cells,
    receptor_cells,
    aggregate_map,
    coarse_inverse,
    coarse_couplings,
):
    masks = overset_masks(donor_cells, receptor_cells, overset_weight)
    krylov = [right_side]
    for j in range(STEPS):
        applied = operate(krylov[j], jacobi_inverse, block_couplings, masks)
        krylov.append((applied - shift_value(j, STEPS) * krylov[j]) / BASIS_SCALE)
    stacked = jnp.stack(krylov)
    local_gram = jnp.einsum("iabc,jabc->ij", stacked, stacked, precision=lax.Precision.HIGHEST)
    gram_total = gathered_sum(gathered_sum(local_gram, "dev"), "group")
    coeffs, thetas = small_solve(gram_total)
    combined = jnp.einsum("i,iabc->abc", coeffs, stacked[:STEPS], precision=lax.Precision.HIGHEST)
    krylov_update = block_apply(jacobi_inverse, combined)
    applied_combined = sum(
        coeffs[j] * (BASIS_SCALE * krylov[j + 1] + thetas[j] * krylov[j]) for j in range(STEPS)
    )
    new_residual = right_side - applied_combined
    agg_count = coarse_inverse.shape[2]
    local_rhs = restrict_field(new_residual, aggregate_map, agg_count)
    own_vals = block_apply(coarse_inverse, local_rhs)
    for k in range(SWEEPS - 1):
        padded = with_halo(own_vals, ((("group", "dev"), 1),), 1)
        own_vals = block_apply(
            coarse_inverse,
            local_rhs
            - block_apply(coarse_couplings[0], padded[:, :-2])
            - block_apply(coarse_couplings[1], padded[:, 2:]),
        )
    update = krylov_update + prolong_field(own_vals, aggregate_map)
    return (update, new_residual)


def solution(mesh):
    return jax.shard_map(
        body,
        mesh=mesh,
        in_specs=(
            P(None, ("group", "dev"), None),
            P(None, None, ("group", "dev"), None),
            P(None, None, None, ("group", "dev"), None),
            P(("group", "dev"), None),
            P(("group", "dev"), None),
            P(("group", "dev"), None),
            P(("group", "dev"), None),
            P(None, None, ("group", "dev")),
            P(None, None, None, ("group", "dev")),
        ),
        out_specs=(P(None, ("group", "dev"), None), P(None, ("group", "dev"), None)),
        check_vma=False,
    )
```

```python
import math

import jax
import jax.numpy as jnp
from jax import lax
from jax.experimental import pallas as pl
from jax.sharding import PartitionSpec as P

STEPS = 8
SWEEPS = 4


BASIS_SCALE = 0.5


def with_halo(cells, sides, width):
    for axis, dim in sides:
        count = lax.axis_size(axis)
        ends = count - 1
        head = lax.slice_in_dim(cells, 0, width, axis=dim)
        tail = lax.slice_in_dim(cells, cells.shape[dim] - width, cells.shape[dim], axis=dim)
        cells = jnp.concatenate(
            [
                lax.ppermute(tail, axis, [(i, (i + 1) % count) for i in range(ends)]),
                cells,
                lax.ppermute(head, axis, [((i + 1) % count, i) for i in range(ends)]),
            ],
            axis=dim,
        )
    return cells


def gathered_sum(values, axis):
    count = lax.axis_size(axis)
    copies = jnp.broadcast_to(values[None], (count,) + values.shape)
    return jnp.sum(lax.all_to_all(copies, axis, 0, 0, tiled=True), axis=0)


def block_apply(blocks, vector):
    return jnp.sum(blocks * vector[None], axis=1)


def shift_value(j, count):
    half_index = j // 2
    point = half_index if j % 2 == 0 else count - 1 - half_index
    return 1.0 + 0.5 * math.cos(math.pi * (2 * point + 1) / (2 * count))


def least_squares_kernel(hessenberg_ref, target_ref, coeffs_ref):
    hessenberg = hessenberg_ref[...]
    target = target_ref[...]
    count = hessenberg.shape[1]
    ortho_cols = []
    triangle = {}
    for j in range(count):
        column = hessenberg[:, j : j + 1]
        for i in range(j):
            factor_ij = jnp.sum(ortho_cols[i] * column, axis=0, keepdims=True)
            triangle[i, j] = factor_ij
            column = column - factor_ij * ortho_cols[i]
        length_val = jnp.sqrt(jnp.sum(column * column, axis=0, keepdims=True))
        triangle[j, j] = length_val
        ortho_cols.append(column / length_val)
    projected = [jnp.sum(q * target, axis=0, keepdims=True) for q in ortho_cols]
    solved = [None] * count
    for j in reversed(range(count)):
        running = projected[j]
        for i in range(j + 1, count):
            running = running - triangle[j, i] * solved[i]
        solved[j] = running / triangle[j, j]
    lanes = lax.broadcasted_iota(jnp.int32, (1, count), 1)
    coeffs = jnp.zeros((1, count), jnp.float32)
    for j in range(count):
        coeffs = jnp.where(lanes == j, solved[j], coeffs)
    coeffs_ref[...] = coeffs


def small_solve(gram_matrix):
    count = gram_matrix.shape[0] - 1
    factor = jnp.transpose(jnp.linalg.cholesky(gram_matrix))
    thetas = jnp.array([shift_value(j, count) for j in range(count)], jnp.float32)
    hessenberg = factor[:, :count] * thetas[None, :] + BASIS_SCALE * factor[:, 1:]
    target = factor[:, :1]
    coeffs = pl.pallas_call(
        least_squares_kernel,
        out_shape=jax.ShapeDtypeStruct((1, count), jnp.float32),
    )(hessenberg, target)
    return (coeffs[0], thetas)


SPLIT = 64


def overset_masks(donor_cells, receptor_cells, overset_weight):
    digits = jnp.arange(SPLIT, dtype=jnp.int32)[:, None]
    donors = donor_cells.reshape(1, -1)
    receptors = receptor_cells.reshape(1, -1)
    weights = overset_weight.reshape(1, -1)
    donor_hi = (donors // SPLIT == digits).astype(jnp.float32)
    donor_lo = (donors % SPLIT == digits).astype(jnp.float32)
    receptor_hi = (receptors // SPLIT == digits).astype(jnp.float32)
    receptor_lo = jnp.where(receptors % SPLIT == digits, weights, 0.0)
    return donor_hi, donor_lo, receptor_hi, receptor_lo


def operate(field, jacobi_inverse, block_couplings, masks):
    donor_hi, donor_lo, receptor_hi, receptor_lo = masks
    scaled = block_apply(jacobi_inverse, field)
    padded = with_halo(scaled, ((("group", "dev"), 1),), 1)
    result = field + block_apply(block_couplings[0], jnp.roll(scaled, 1, axis=2))
    result = result + block_apply(block_couplings[1], jnp.roll(scaled, -1, axis=2))
    result = result + block_apply(block_couplings[2], padded[:, :-2])
    result = result + block_apply(block_couplings[3], padded[:, 2:])
    comps = scaled.shape[0]
    split_vals = scaled.reshape(comps, -1, SPLIT)
    partial = jnp.einsum("chl,hs->cls", split_vals, donor_hi, precision=lax.Precision.HIGHEST)
    outgoing = jnp.sum(partial * donor_lo[None], axis=1)
    outgoing = outgoing.reshape(comps, lax.axis_size("dev"), -1)
    incoming = lax.all_to_all(outgoing, "dev", split_axis=1, concat_axis=1, tiled=True)
    incoming = incoming.reshape(comps, 1, -1)
    spread = incoming * receptor_lo[None]
    moved = jnp.einsum("hs,cls->chl", receptor_hi, spread, precision=lax.Precision.HIGHEST)
    return result - moved.reshape(result.shape)


def layer_onehot(labels, count):
    return (labels[:, None] == jnp.arange(count, dtype=jnp.int32)[None, :]).astype(jnp.float32)


def restrict_field(field, aggregate_map, count):
    totals = jnp.zeros((field.shape[0], count), jnp.float32)
    for k in range(field.shape[1]):
        totals = totals + jnp.dot(
            field[:, k], layer_onehot(aggregate_map[k], count), precision=lax.Precision.HIGHEST
        )
    return totals


def prolong_field(coarse_vals, aggregate_map):
    count = coarse_vals.shape[1]
    layers_out = [
        jnp.dot(
            coarse_vals,
            jnp.transpose(layer_onehot(aggregate_map[k], count)),
            precision=lax.Precision.HIGHEST,
        )
        for k in range(aggregate_map.shape[0])
    ]
    return jnp.stack(layers_out, axis=1)


def body(
    right_side,
    jacobi_inverse,
    block_couplings,
    overset_weight,
    donor_cells,
    receptor_cells,
    aggregate_map,
    coarse_inverse,
    coarse_couplings,
):
    masks = overset_masks(donor_cells, receptor_cells, overset_weight)
    krylov = [right_side]
    for j in range(STEPS):
        applied = operate(krylov[j], jacobi_inverse, block_couplings, masks)
        krylov.append((applied - shift_value(j, STEPS) * krylov[j]) / BASIS_SCALE)
    stacked = jnp.stack(krylov)
    local_gram = jnp.einsum("iabc,jabc->ij", stacked, stacked, precision=lax.Precision.HIGHEST)
    gram_total = gathered_sum(gathered_sum(local_gram, "dev"), "group")
    coeffs, thetas = small_solve(gram_total)
    combined = jnp.einsum("i,iabc->abc", coeffs, stacked[:STEPS], precision=lax.Precision.HIGHEST)
    krylov_update = block_apply(jacobi_inverse, combined)
    applied_combined = sum(
        coeffs[j] * (BASIS_SCALE * krylov[j + 1] + thetas[j] * krylov[j]) for j in range(STEPS)
    )
    new_residual = right_side - applied_combined
    agg_count = coarse_inverse.shape[2]
    local_rhs = restrict_field(new_residual, aggregate_map, agg_count)
    reach = SWEEPS - 1
    sides = ((("group", "dev"), 1),)
    wide_rhs = with_halo(local_rhs, sides, reach)
    wide_inverse = with_halo(coarse_inverse, ((("group", "dev"), 2),), reach)
    wide_couplings = with_halo(coarse_couplings, ((("group", "dev"), 3),), reach)
    wide_vals = block_apply(wide_inverse, wide_rhs)
    for k in range(SWEEPS - 1):
        zero_col = jnp.zeros_like(wide_vals[:, :1])
        left_vals = jnp.concatenate([zero_col, wide_vals[:, :-1]], axis=1)
        right_vals = jnp.concatenate([wide_vals[:, 1:], zero_col], axis=1)
        wide_vals = block_apply(
            wide_inverse,
            wide_rhs
            - block_apply(wide_couplings[0], left_vals)
            - block_apply(wide_couplings[1], right_vals),
        )
    own_vals = wide_vals[:, reach : wide_vals.shape[1] - reach]
    update = krylov_update + prolong_field(own_vals, aggregate_map)
    return (update, new_residual)


def solution(mesh):
    return jax.shard_map(
        body,
        mesh=mesh,
        in_specs=(
            P(None, ("group", "dev"), None),
            P(None, None, ("group", "dev"), None),
            P(None, None, None, ("group", "dev"), None),
            P(("group", "dev"), None),
            P(("group", "dev"), None),
            P(("group", "dev"), None),
            P(("group", "dev"), None),
            P(None, None, ("group", "dev")),
            P(None, None, None, ("group", "dev")),
        ),
        out_specs=(P(None, ("group", "dev"), None), P(None, ("group", "dev"), None)),
        check_vma=False,
    )
```

```python
import math

import jax
import jax.numpy as jnp
from jax import lax
from jax.experimental import pallas as pl
from jax.sharding import PartitionSpec as P

STEPS = 8
SWEEPS = 4


BASIS_SCALE = 0.5


def with_halo(cells, sides, width):
    for axis, dim in sides:
        count = lax.axis_size(axis)
        ends = count - 1
        head = lax.slice_in_dim(cells, 0, width, axis=dim)
        tail = lax.slice_in_dim(cells, cells.shape[dim] - width, cells.shape[dim], axis=dim)
        cells = jnp.concatenate(
            [
                lax.ppermute(tail, axis, [(i, (i + 1) % count) for i in range(ends)]),
                cells,
                lax.ppermute(head, axis, [((i + 1) % count, i) for i in range(ends)]),
            ],
            axis=dim,
        )
    return cells


def gathered_sum(values, axis):
    count = lax.axis_size(axis)
    copies = jnp.broadcast_to(values[None], (count,) + values.shape)
    return jnp.sum(lax.all_to_all(copies, axis, 0, 0, tiled=True), axis=0)


def block_apply(blocks, vector):
    return jnp.sum(blocks * vector[None], axis=1)


def shift_value(j, count):
    half_index = j // 2
    point = half_index if j % 2 == 0 else count - 1 - half_index
    return 1.0 + 0.5 * math.cos(math.pi * (2 * point + 1) / (2 * count))


def least_squares_kernel(hessenberg_ref, target_ref, coeffs_ref):
    hessenberg = hessenberg_ref[...]
    target = target_ref[...]
    count = hessenberg.shape[1]
    ortho_cols = []
    triangle = {}
    for j in range(count):
        column = hessenberg[:, j : j + 1]
        for i in range(j):
            factor_ij = jnp.sum(ortho_cols[i] * column, axis=0, keepdims=True)
            triangle[i, j] = factor_ij
            column = column - factor_ij * ortho_cols[i]
        length_val = jnp.sqrt(jnp.sum(column * column, axis=0, keepdims=True))
        triangle[j, j] = length_val
        ortho_cols.append(column / length_val)
    projected = [jnp.sum(q * target, axis=0, keepdims=True) for q in ortho_cols]
    solved = [None] * count
    for j in reversed(range(count)):
        running = projected[j]
        for i in range(j + 1, count):
            running = running - triangle[j, i] * solved[i]
        solved[j] = running / triangle[j, j]
    lanes = lax.broadcasted_iota(jnp.int32, (1, count), 1)
    coeffs = jnp.zeros((1, count), jnp.float32)
    for j in range(count):
        coeffs = jnp.where(lanes == j, solved[j], coeffs)
    coeffs_ref[...] = coeffs


def small_solve(gram_matrix):
    count = gram_matrix.shape[0] - 1
    factor = jnp.transpose(jnp.linalg.cholesky(gram_matrix))
    thetas = jnp.array([shift_value(j, count) for j in range(count)], jnp.float32)
    hessenberg = factor[:, :count] * thetas[None, :] + BASIS_SCALE * factor[:, 1:]
    target = factor[:, :1]
    coeffs = pl.pallas_call(
        least_squares_kernel,
        out_shape=jax.ShapeDtypeStruct((1, count), jnp.float32),
    )(hessenberg, target)
    return (coeffs[0], thetas)


LANES = 128


def overset_masks(donor_cells, receptor_cells, overset_weight, rows):
    lane_ids = jnp.arange(LANES, dtype=jnp.int32)[:, None]
    row_ids = jnp.arange(rows, dtype=jnp.int32)[:, None]
    donors = donor_cells.reshape(1, -1)
    receptors = receptor_cells.reshape(1, -1)
    weights = overset_weight.reshape(1, -1)
    donor_lane = (donors % LANES == lane_ids).astype(jnp.float32)
    donor_row = (donors // LANES == row_ids).astype(jnp.float32)
    receptor_lane = (receptors % LANES == lane_ids).astype(jnp.float32)
    receptor_row = jnp.where(receptors // LANES == row_ids, weights, 0.0)
    return donor_lane, donor_row, receptor_lane, receptor_row


def loop_roll(values, shift):
    lane_axis = values.ndim - 1
    lanes = lax.broadcasted_iota(jnp.int32, values.shape, lane_axis)
    lane_rolled = jnp.roll(values, shift, axis=lane_axis)
    carried = jnp.roll(lane_rolled, shift, axis=lane_axis - 1)
    edge = 0 if shift > 0 else values.shape[lane_axis] - 1
    return jnp.where(lanes == edge, carried, lane_rolled)


def operate(field, jacobi_inverse, block_couplings, masks):
    donor_lane, donor_row, receptor_lane, receptor_row = masks
    scaled = block_apply(jacobi_inverse, field)
    padded = with_halo(scaled, ((("group", "dev"), 1),), 1)
    result = field + block_apply(block_couplings[0], loop_roll(scaled, 1))
    result = result + block_apply(block_couplings[1], loop_roll(scaled, -1))
    result = result + block_apply(block_couplings[2], padded[:, :-2])
    result = result + block_apply(block_couplings[3], padded[:, 2:])
    comps = scaled.shape[0]
    split_vals = scaled.reshape(comps, -1, LANES)
    partial = jnp.einsum("chl,ls->chs", split_vals, donor_lane, precision=lax.Precision.HIGHEST)
    outgoing = jnp.sum(partial * donor_row[None], axis=1)
    outgoing = outgoing.reshape(comps, lax.axis_size("dev"), -1)
    incoming = lax.all_to_all(outgoing, "dev", split_axis=1, concat_axis=1, tiled=True)
    incoming = incoming.reshape(comps, 1, -1)
    spread = incoming * receptor_row[None]
    moved = jnp.einsum("chs,ls->chl", spread, receptor_lane, precision=lax.Precision.HIGHEST)
    return result - moved.reshape(result.shape)


def layer_onehot(labels, count):
    return (labels[:, None] == jnp.arange(count, dtype=jnp.int32)[None, :]).astype(jnp.float32)


def restrict_field(field, aggregate_map, count):
    totals = jnp.zeros((field.shape[0], count), jnp.float32)
    for k in range(field.shape[1]):
        totals = totals + jnp.dot(
            field[:, k], layer_onehot(aggregate_map[k], count), precision=lax.Precision.HIGHEST
        )
    return totals


def prolong_field(coarse_vals, aggregate_map):
    count = coarse_vals.shape[1]
    layers_out = [
        jnp.dot(
            coarse_vals,
            jnp.transpose(layer_onehot(aggregate_map[k], count)),
            precision=lax.Precision.HIGHEST,
        )
        for k in range(aggregate_map.shape[0])
    ]
    return jnp.stack(layers_out, axis=1)


def body(
    right_side,
    jacobi_inverse,
    block_couplings,
    overset_weight,
    donor_cells,
    receptor_cells,
    aggregate_map,
    coarse_inverse,
    coarse_couplings,
):
    comps, layers, plane = right_side.shape
    tiled = (layers, plane // LANES, LANES)
    masks = overset_masks(donor_cells, receptor_cells, overset_weight, layers * plane // LANES)
    dense_rhs = right_side.reshape((comps,) + tiled)
    dense_inverse = jacobi_inverse.reshape(jacobi_inverse.shape[:2] + tiled)
    dense_couplings = block_couplings.reshape(block_couplings.shape[:3] + tiled)
    krylov = [dense_rhs]
    for j in range(STEPS):
        applied = operate(krylov[j], dense_inverse, dense_couplings, masks)
        krylov.append((applied - shift_value(j, STEPS) * krylov[j]) / BASIS_SCALE)
    stacked = jnp.stack(krylov)
    local_gram = jnp.einsum("iabcd,jabcd->ij", stacked, stacked, precision=lax.Precision.HIGHEST)
    gram_total = gathered_sum(gathered_sum(local_gram, "dev"), "group")
    coeffs, thetas = small_solve(gram_total)
    combined = jnp.einsum("i,iabcd->abcd", coeffs, stacked[:STEPS], precision=lax.Precision.HIGHEST)
    krylov_update = block_apply(dense_inverse, combined).reshape(right_side.shape)
    applied_combined = sum(
        coeffs[j] * (BASIS_SCALE * krylov[j + 1] + thetas[j] * krylov[j]) for j in range(STEPS)
    )
    new_residual = (dense_rhs - applied_combined).reshape(right_side.shape)
    agg_count = coarse_inverse.shape[2]
    local_rhs = restrict_field(new_residual, aggregate_map, agg_count)
    reach = SWEEPS - 1
    sides = ((("group", "dev"), 1),)
    wide_rhs = with_halo(local_rhs, sides, reach)
    wide_inverse = with_halo(coarse_inverse, ((("group", "dev"), 2),), reach)
    wide_couplings = with_halo(coarse_couplings, ((("group", "dev"), 3),), reach)
    wide_vals = block_apply(wide_inverse, wide_rhs)
    for k in range(SWEEPS - 1):
        zero_col = jnp.zeros_like(wide_vals[:, :1])
        left_vals = jnp.concatenate([zero_col, wide_vals[:, :-1]], axis=1)
        right_vals = jnp.concatenate([wide_vals[:, 1:], zero_col], axis=1)
        wide_vals = block_apply(
            wide_inverse,
            wide_rhs
            - block_apply(wide_couplings[0], left_vals)
            - block_apply(wide_couplings[1], right_vals),
        )
    own_vals = wide_vals[:, reach : wide_vals.shape[1] - reach]
    update = krylov_update + prolong_field(own_vals, aggregate_map)
    return (update, new_residual)


def solution(mesh):
    return jax.shard_map(
        body,
        mesh=mesh,
        in_specs=(
            P(None, ("group", "dev"), None),
            P(None, None, ("group", "dev"), None),
            P(None, None, None, ("group", "dev"), None),
            P(("group", "dev"), None),
            P(("group", "dev"), None),
            P(("group", "dev"), None),
            P(("group", "dev"), None),
            P(None, None, ("group", "dev")),
            P(None, None, None, ("group", "dev")),
        ),
        out_specs=(P(None, ("group", "dev"), None), P(None, ("group", "dev"), None)),
        check_vma=False,
    )
```

```python
import math

import jax
import jax.numpy as jnp
from jax import lax
from jax.experimental import pallas as pl
from jax.sharding import PartitionSpec as P

STEPS = 8
SWEEPS = 4


BASIS_SCALE = 0.5


def with_halo(cells, sides, width):
    for axis, dim in sides:
        count = lax.axis_size(axis)
        ends = count - 1
        head = lax.slice_in_dim(cells, 0, width, axis=dim)
        tail = lax.slice_in_dim(cells, cells.shape[dim] - width, cells.shape[dim], axis=dim)
        cells = jnp.concatenate(
            [
                lax.ppermute(tail, axis, [(i, (i + 1) % count) for i in range(ends)]),
                cells,
                lax.ppermute(head, axis, [((i + 1) % count, i) for i in range(ends)]),
            ],
            axis=dim,
        )
    return cells


def gathered_sum(values, axis):
    count = lax.axis_size(axis)
    copies = jnp.broadcast_to(values[None], (count,) + values.shape)
    return jnp.sum(lax.all_to_all(copies, axis, 0, 0, tiled=True), axis=0)


def block_apply(blocks, vector):
    total = blocks[:, 0] * vector[0]
    for m in range(1, blocks.shape[1]):
        total = total + blocks[:, m] * vector[m]
    return total


def shift_value(j, count):
    half_index = j // 2
    point = half_index if j % 2 == 0 else count - 1 - half_index
    return 1.0 + 0.5 * math.cos(math.pi * (2 * point + 1) / (2 * count))


def least_squares_kernel(hessenberg_ref, target_ref, coeffs_ref):
    hessenberg = hessenberg_ref[...]
    target = target_ref[...]
    count = hessenberg.shape[1]
    ortho_cols = []
    triangle = {}
    for j in range(count):
        column = hessenberg[:, j : j + 1]
        for i in range(j):
            factor_ij = jnp.sum(ortho_cols[i] * column, axis=0, keepdims=True)
            triangle[i, j] = factor_ij
            column = column - factor_ij * ortho_cols[i]
        length_val = jnp.sqrt(jnp.sum(column * column, axis=0, keepdims=True))
        triangle[j, j] = length_val
        ortho_cols.append(column / length_val)
    projected = [jnp.sum(q * target, axis=0, keepdims=True) for q in ortho_cols]
    solved = [None] * count
    for j in reversed(range(count)):
        running = projected[j]
        for i in range(j + 1, count):
            running = running - triangle[j, i] * solved[i]
        solved[j] = running / triangle[j, j]
    lanes = lax.broadcasted_iota(jnp.int32, (1, count), 1)
    coeffs = jnp.zeros((1, count), jnp.float32)
    for j in range(count):
        coeffs = jnp.where(lanes == j, solved[j], coeffs)
    coeffs_ref[...] = coeffs


def small_solve(gram_matrix):
    count = gram_matrix.shape[0] - 1
    factor = jnp.transpose(jnp.linalg.cholesky(gram_matrix))
    thetas = jnp.array([shift_value(j, count) for j in range(count)], jnp.float32)
    hessenberg = factor[:, :count] * thetas[None, :] + BASIS_SCALE * factor[:, 1:]
    target = factor[:, :1]
    coeffs = pl.pallas_call(
        least_squares_kernel,
        out_shape=jax.ShapeDtypeStruct((1, count), jnp.float32),
    )(hessenberg, target)
    return (coeffs[0], thetas)


LANES = 128


def overset_masks(donor_cells, receptor_cells, overset_weight, rows):
    lane_ids = jnp.arange(LANES, dtype=jnp.int32)[:, None]
    row_ids = jnp.arange(rows, dtype=jnp.int32)[:, None]
    donors = donor_cells.reshape(1, -1)
    receptors = receptor_cells.reshape(1, -1)
    weights = overset_weight.reshape(1, -1)
    donor_lane = (donors % LANES == lane_ids).astype(jnp.float32)
    donor_row = (donors // LANES == row_ids).astype(jnp.float32)
    receptor_lane = (receptors % LANES == lane_ids).astype(jnp.float32)
    receptor_row = jnp.where(receptors // LANES == row_ids, weights, 0.0)
    return donor_lane, donor_row, receptor_lane, receptor_row


def loop_roll(values, shift):
    lane_axis = values.ndim - 1
    lanes = lax.broadcasted_iota(jnp.int32, values.shape, lane_axis)
    lane_rolled = jnp.roll(values, shift, axis=lane_axis)
    carried = jnp.roll(lane_rolled, shift, axis=lane_axis - 1)
    edge = 0 if shift > 0 else values.shape[lane_axis] - 1
    return jnp.where(lanes == edge, carried, lane_rolled)


def operate(field, jacobi_inverse, block_couplings, masks):
    donor_lane, donor_row, receptor_lane, receptor_row = masks
    scaled = block_apply(jacobi_inverse, field)
    padded = with_halo(scaled, ((("group", "dev"), 1),), 1)
    result = field + block_apply(block_couplings[0], loop_roll(scaled, 1))
    result = result + block_apply(block_couplings[1], loop_roll(scaled, -1))
    result = result + block_apply(block_couplings[2], padded[:, :-2])
    result = result + block_apply(block_couplings[3], padded[:, 2:])
    comps = scaled.shape[0]
    split_vals = scaled.reshape(comps, -1, LANES)
    partial = jnp.einsum("chl,ls->chs", split_vals, donor_lane, precision=lax.Precision.HIGHEST)
    outgoing = jnp.sum(partial * donor_row[None], axis=1)
    outgoing = outgoing.reshape(comps, lax.axis_size("dev"), -1)
    incoming = lax.all_to_all(outgoing, "dev", split_axis=1, concat_axis=1, tiled=True)
    incoming = incoming.reshape(comps, 1, -1)
    spread = incoming * receptor_row[None]
    moved = jnp.einsum("chs,ls->chl", spread, receptor_lane, precision=lax.Precision.HIGHEST)
    return result - moved.reshape(result.shape)


def layer_onehot(labels, count):
    return (labels[:, None] == jnp.arange(count, dtype=jnp.int32)[None, :]).astype(jnp.float32)


def restrict_field(field, aggregate_map, count):
    totals = jnp.zeros((field.shape[0], count), jnp.float32)
    for k in range(field.shape[1]):
        totals = totals + jnp.dot(
            field[:, k], layer_onehot(aggregate_map[k], count), precision=lax.Precision.HIGHEST
        )
    return totals


def prolong_field(coarse_vals, aggregate_map):
    count = coarse_vals.shape[1]
    layers_out = [
        jnp.dot(
            coarse_vals,
            jnp.transpose(layer_onehot(aggregate_map[k], count)),
            precision=lax.Precision.HIGHEST,
        )
        for k in range(aggregate_map.shape[0])
    ]
    return jnp.stack(layers_out, axis=1)


def body(
    right_side,
    jacobi_inverse,
    block_couplings,
    overset_weight,
    donor_cells,
    receptor_cells,
    aggregate_map,
    coarse_inverse,
    coarse_couplings,
):
    comps, layers, plane = right_side.shape
    tiled = (layers, plane // LANES, LANES)
    masks = overset_masks(donor_cells, receptor_cells, overset_weight, layers * plane // LANES)
    dense_rhs = right_side.reshape((comps,) + tiled)
    dense_inverse = jacobi_inverse.reshape(jacobi_inverse.shape[:2] + tiled)
    dense_couplings = block_couplings.reshape(block_couplings.shape[:3] + tiled)
    krylov = [dense_rhs]
    for j in range(STEPS):
        applied = operate(krylov[j], dense_inverse, dense_couplings, masks)
        krylov.append((applied - shift_value(j, STEPS) * krylov[j]) / BASIS_SCALE)
    stacked = jnp.stack(krylov)
    local_gram = jnp.einsum("iabcd,jabcd->ij", stacked, stacked, precision=lax.Precision.HIGHEST)
    gram_total = gathered_sum(gathered_sum(local_gram, "dev"), "group")
    coeffs, thetas = small_solve(gram_total)
    combined = jnp.einsum("i,iabcd->abcd", coeffs, stacked[:STEPS], precision=lax.Precision.HIGHEST)
    krylov_update = block_apply(dense_inverse, combined).reshape(right_side.shape)
    applied_combined = sum(
        coeffs[j] * (BASIS_SCALE * krylov[j + 1] + thetas[j] * krylov[j]) for j in range(STEPS)
    )
    new_residual = (dense_rhs - applied_combined).reshape(right_side.shape)
    agg_count = coarse_inverse.shape[2]
    local_rhs = restrict_field(new_residual, aggregate_map, agg_count)
    reach = SWEEPS - 1
    sides = ((("group", "dev"), 1),)
    wide_rhs = with_halo(local_rhs, sides, reach)
    wide_inverse = with_halo(coarse_inverse, ((("group", "dev"), 2),), reach)
    wide_couplings = with_halo(coarse_couplings, ((("group", "dev"), 3),), reach)
    wide_vals = block_apply(wide_inverse, wide_rhs)
    for k in range(SWEEPS - 1):
        zero_col = jnp.zeros_like(wide_vals[:, :1])
        left_vals = jnp.concatenate([zero_col, wide_vals[:, :-1]], axis=1)
        right_vals = jnp.concatenate([wide_vals[:, 1:], zero_col], axis=1)
        wide_vals = block_apply(
            wide_inverse,
            wide_rhs
            - block_apply(wide_couplings[0], left_vals)
            - block_apply(wide_couplings[1], right_vals),
        )
    own_vals = wide_vals[:, reach : wide_vals.shape[1] - reach]
    update = krylov_update + prolong_field(own_vals, aggregate_map)
    return (update, new_residual)


def solution(mesh):
    return jax.shard_map(
        body,
        mesh=mesh,
        in_specs=(
            P(None, ("group", "dev"), None),
            P(None, None, ("group", "dev"), None),
            P(None, None, None, ("group", "dev"), None),
            P(("group", "dev"), None),
            P(("group", "dev"), None),
            P(("group", "dev"), None),
            P(("group", "dev"), None),
            P(None, None, ("group", "dev")),
            P(None, None, None, ("group", "dev")),
        ),
        out_specs=(P(None, ("group", "dev"), None), P(None, ("group", "dev"), None)),
        check_vma=False,
    )
```

```python
import math

import jax
import jax.numpy as jnp
from jax import lax
from jax.experimental import pallas as pl
from jax.sharding import PartitionSpec as P

STEPS = 8
SWEEPS = 4


BASIS_SCALE = 0.5


def with_halo(cells, sides, width):
    for axis, dim in sides:
        count = lax.axis_size(axis)
        ends = count - 1
        head = lax.slice_in_dim(cells, 0, width, axis=dim)
        tail = lax.slice_in_dim(cells, cells.shape[dim] - width, cells.shape[dim], axis=dim)
        cells = jnp.concatenate(
            [
                lax.ppermute(tail, axis, [(i, (i + 1) % count) for i in range(ends)]),
                cells,
                lax.ppermute(head, axis, [((i + 1) % count, i) for i in range(ends)]),
            ],
            axis=dim,
        )
    return cells


def gathered_sum(values, axis):
    count = lax.axis_size(axis)
    copies = jnp.broadcast_to(values[None], (count,) + values.shape)
    return jnp.sum(lax.all_to_all(copies, axis, 0, 0, tiled=True), axis=0)


def block_apply(blocks, vector):
    return jnp.sum(blocks * vector[None], axis=1)


def shift_value(j, count):
    half_index = j // 2
    point = half_index if j % 2 == 0 else count - 1 - half_index
    return 1.0 + 0.5 * math.cos(math.pi * (2 * point + 1) / (2 * count))


def least_squares_kernel(hessenberg_ref, target_ref, coeffs_ref):
    hessenberg = hessenberg_ref[...]
    target = target_ref[...]
    count = hessenberg.shape[1]
    ortho_cols = []
    triangle = {}
    for j in range(count):
        column = hessenberg[:, j : j + 1]
        for i in range(j):
            factor_ij = jnp.sum(ortho_cols[i] * column, axis=0, keepdims=True)
            triangle[i, j] = factor_ij
            column = column - factor_ij * ortho_cols[i]
        length_val = jnp.sqrt(jnp.sum(column * column, axis=0, keepdims=True))
        triangle[j, j] = length_val
        ortho_cols.append(column / length_val)
    projected = [jnp.sum(q * target, axis=0, keepdims=True) for q in ortho_cols]
    solved = [None] * count
    for j in reversed(range(count)):
        running = projected[j]
        for i in range(j + 1, count):
            running = running - triangle[j, i] * solved[i]
        solved[j] = running / triangle[j, j]
    lanes = lax.broadcasted_iota(jnp.int32, (1, count), 1)
    coeffs = jnp.zeros((1, count), jnp.float32)
    for j in range(count):
        coeffs = jnp.where(lanes == j, solved[j], coeffs)
    coeffs_ref[...] = coeffs


def small_solve(gram_matrix):
    count = gram_matrix.shape[0] - 1
    factor = jnp.transpose(jnp.linalg.cholesky(gram_matrix))
    thetas = jnp.array([shift_value(j, count) for j in range(count)], jnp.float32)
    hessenberg = factor[:, :count] * thetas[None, :] + BASIS_SCALE * factor[:, 1:]
    target = factor[:, :1]
    coeffs = pl.pallas_call(
        least_squares_kernel,
        out_shape=jax.ShapeDtypeStruct((1, count), jnp.float32),
    )(hessenberg, target)
    return (coeffs[0], thetas)


LANES = 128


def overset_masks(donor_cells, receptor_cells, overset_weight, rows):
    lane_ids = jnp.arange(LANES, dtype=jnp.int32)[:, None]
    row_ids = jnp.arange(rows, dtype=jnp.int32)[:, None]
    donors = donor_cells.reshape(1, -1)
    receptors = receptor_cells.reshape(1, -1)
    weights = overset_weight.reshape(1, -1)
    donor_lane = (donors % LANES == lane_ids).astype(jnp.float32)
    donor_row = (donors // LANES == row_ids).astype(jnp.float32)
    receptor_lane = (receptors % LANES == lane_ids).astype(jnp.float32)
    receptor_row = jnp.where(receptors // LANES == row_ids, weights, 0.0)
    return donor_lane, donor_row, receptor_lane, receptor_row


def loop_roll(values, shift):
    lane_axis = values.ndim - 1
    lanes = lax.broadcasted_iota(jnp.int32, values.shape, lane_axis)
    lane_rolled = jnp.roll(values, shift, axis=lane_axis)
    carried = jnp.roll(lane_rolled, shift, axis=lane_axis - 1)
    edge = 0 if shift > 0 else values.shape[lane_axis] - 1
    return jnp.where(lanes == edge, carried, lane_rolled)


def operate(field, jacobi_inverse, block_couplings, masks):
    donor_lane, donor_row, receptor_lane, receptor_row = masks
    scaled = block_apply(jacobi_inverse, field)
    padded = with_halo(scaled, ((("group", "dev"), 1),), 1)
    result = field + block_apply(block_couplings[0], loop_roll(scaled, 1))
    result = result + block_apply(block_couplings[1], loop_roll(scaled, -1))
    result = result + block_apply(block_couplings[2], padded[:, :-2])
    result = result + block_apply(block_couplings[3], padded[:, 2:])
    comps = scaled.shape[0]
    split_vals = scaled.reshape(comps, -1, LANES)
    partial = jnp.einsum("chl,ls->chs", split_vals, donor_lane, precision=lax.Precision.HIGHEST)
    outgoing = jnp.sum(partial * donor_row[None], axis=1)
    outgoing = outgoing.reshape(comps, lax.axis_size("dev"), -1)
    incoming = lax.all_to_all(outgoing, "dev", split_axis=1, concat_axis=1, tiled=True)
    incoming = incoming.reshape(comps, 1, -1)
    spread = incoming * receptor_row[None]
    moved = jnp.einsum("chs,ls->chl", spread, receptor_lane, precision=lax.Precision.HIGHEST)
    return result - moved.reshape(result.shape)


def layer_onehot(labels, count):
    return (labels[:, None] == jnp.arange(count, dtype=jnp.int32)[None, :]).astype(jnp.float32)


def restrict_field(field, aggregate_map, count):
    totals = jnp.zeros((field.shape[0], count), jnp.float32)
    for k in range(field.shape[1]):
        totals = totals + jnp.dot(
            field[:, k], layer_onehot(aggregate_map[k], count), precision=lax.Precision.HIGHEST
        )
    return totals


def prolong_field(coarse_vals, aggregate_map):
    count = coarse_vals.shape[1]
    layers_out = [
        jnp.dot(
            coarse_vals,
            jnp.transpose(layer_onehot(aggregate_map[k], count)),
            precision=lax.Precision.HIGHEST,
        )
        for k in range(aggregate_map.shape[0])
    ]
    return jnp.stack(layers_out, axis=1)


def body(
    right_side,
    jacobi_inverse,
    block_couplings,
    overset_weight,
    donor_cells,
    receptor_cells,
    aggregate_map,
    coarse_inverse,
    coarse_couplings,
):
    comps, layers, plane = right_side.shape
    tiled = (layers, plane // LANES, LANES)
    masks = overset_masks(donor_cells, receptor_cells, overset_weight, layers * plane // LANES)
    dense_rhs = right_side.reshape((comps,) + tiled)
    dense_inverse = jacobi_inverse.reshape(jacobi_inverse.shape[:2] + tiled)
    dense_couplings = block_couplings.reshape(block_couplings.shape[:3] + tiled)
    krylov = [dense_rhs]
    for j in range(STEPS):
        applied = operate(krylov[j], dense_inverse, dense_couplings, masks)
        krylov.append((applied - shift_value(j, STEPS) * krylov[j]) / BASIS_SCALE)
    stacked = jnp.stack(krylov)
    local_gram = jnp.einsum("iabcd,jabcd->ij", stacked, stacked, precision=lax.Precision.HIGHEST)
    gram_total = gathered_sum(gathered_sum(local_gram, "dev"), "group")
    coeffs, thetas = small_solve(gram_total)
    combined = sum(coeffs[j] * krylov[j] for j in range(STEPS))
    krylov_update = block_apply(dense_inverse, combined).reshape(right_side.shape)
    applied_combined = sum(
        coeffs[j] * (BASIS_SCALE * krylov[j + 1] + thetas[j] * krylov[j]) for j in range(STEPS)
    )
    new_residual = (dense_rhs - applied_combined).reshape(right_side.shape)
    agg_count = coarse_inverse.shape[2]
    local_rhs = restrict_field(new_residual, aggregate_map, agg_count)
    reach = SWEEPS - 1
    sides = ((("group", "dev"), 1),)
    wide_rhs = with_halo(local_rhs, sides, reach)
    wide_inverse = with_halo(coarse_inverse, ((("group", "dev"), 2),), reach)
    wide_couplings = with_halo(coarse_couplings, ((("group", "dev"), 3),), reach)
    wide_vals = block_apply(wide_inverse, wide_rhs)
    for k in range(SWEEPS - 1):
        zero_col = jnp.zeros_like(wide_vals[:, :1])
        left_vals = jnp.concatenate([zero_col, wide_vals[:, :-1]], axis=1)
        right_vals = jnp.concatenate([wide_vals[:, 1:], zero_col], axis=1)
        wide_vals = block_apply(
            wide_inverse,
            wide_rhs
            - block_apply(wide_couplings[0], left_vals)
            - block_apply(wide_couplings[1], right_vals),
        )
    own_vals = wide_vals[:, reach : wide_vals.shape[1] - reach]
    update = krylov_update + prolong_field(own_vals, aggregate_map)
    return (update, new_residual)


def solution(mesh):
    return jax.shard_map(
        body,
        mesh=mesh,
        in_specs=(
            P(None, ("group", "dev"), None),
            P(None, None, ("group", "dev"), None),
            P(None, None, None, ("group", "dev"), None),
            P(("group", "dev"), None),
            P(("group", "dev"), None),
            P(("group", "dev"), None),
            P(("group", "dev"), None),
            P(None, None, ("group", "dev")),
            P(None, None, None, ("group", "dev")),
        ),
        out_specs=(P(None, ("group", "dev"), None), P(None, ("group", "dev"), None)),
        check_vma=False,
    )
```

```python
import math

import jax
import jax.numpy as jnp
from jax import lax
from jax.experimental import pallas as pl
from jax.sharding import PartitionSpec as P

STEPS = 8
SWEEPS = 4


BASIS_SCALE = 0.5


def with_halo(cells, sides, width):
    for axis, dim in sides:
        count = lax.axis_size(axis)
        ends = count - 1
        head = lax.slice_in_dim(cells, 0, width, axis=dim)
        tail = lax.slice_in_dim(cells, cells.shape[dim] - width, cells.shape[dim], axis=dim)
        cells = jnp.concatenate(
            [
                lax.ppermute(tail, axis, [(i, (i + 1) % count) for i in range(ends)]),
                cells,
                lax.ppermute(head, axis, [((i + 1) % count, i) for i in range(ends)]),
            ],
            axis=dim,
        )
    return cells


def gathered_sum(values, axis):
    count = lax.axis_size(axis)
    copies = jnp.broadcast_to(values[None], (count,) + values.shape)
    return jnp.sum(lax.all_to_all(copies, axis, 0, 0, tiled=True), axis=0)


def block_apply(blocks, vector):
    return jnp.sum(blocks * vector[None], axis=1)


def shift_value(j, count):
    half_index = j // 2
    point = half_index if j % 2 == 0 else count - 1 - half_index
    return 1.0 + 0.5 * math.cos(math.pi * (2 * point + 1) / (2 * count))


def least_squares_kernel(hessenberg_ref, target_ref, coeffs_ref):
    hessenberg = hessenberg_ref[...]
    target = target_ref[...]
    count = hessenberg.shape[1]
    ortho_cols = []
    triangle = {}
    for j in range(count):
        column = hessenberg[:, j : j + 1]
        for i in range(j):
            factor_ij = jnp.sum(ortho_cols[i] * column, axis=0, keepdims=True)
            triangle[i, j] = factor_ij
            column = column - factor_ij * ortho_cols[i]
        length_val = jnp.sqrt(jnp.sum(column * column, axis=0, keepdims=True))
        triangle[j, j] = length_val
        ortho_cols.append(column / length_val)
    projected = [jnp.sum(q * target, axis=0, keepdims=True) for q in ortho_cols]
    solved = [None] * count
    for j in reversed(range(count)):
        running = projected[j]
        for i in range(j + 1, count):
            running = running - triangle[j, i] * solved[i]
        solved[j] = running / triangle[j, j]
    lanes = lax.broadcasted_iota(jnp.int32, (1, count), 1)
    coeffs = jnp.zeros((1, count), jnp.float32)
    for j in range(count):
        coeffs = jnp.where(lanes == j, solved[j], coeffs)
    coeffs_ref[...] = coeffs


def gram_kernel(*refs):
    vector_refs, gram_ref = refs[:-1], refs[-1]
    count = len(vector_refs)
    vectors = [ref[...] for ref in vector_refs]
    rows = lax.broadcasted_iota(jnp.int32, (count, count), 0)
    cols = lax.broadcasted_iota(jnp.int32, (count, count), 1)
    gram = jnp.zeros((count, count), jnp.float32)
    for i in range(count):
        for j in range(i, count):
            product = vectors[i] * vectors[j]
            total = jnp.sum(jnp.sum(product, axis=0, keepdims=True), axis=1, keepdims=True)
            spot = ((rows == i) & (cols == j)) | ((rows == j) & (cols == i))
            gram = jnp.where(spot, total, gram)
    gram_ref[...] = gram


def small_solve(gram_matrix):
    count = gram_matrix.shape[0] - 1
    factor = jnp.transpose(jnp.linalg.cholesky(gram_matrix))
    thetas = jnp.array([shift_value(j, count) for j in range(count)], jnp.float32)
    hessenberg = factor[:, :count] * thetas[None, :] + BASIS_SCALE * factor[:, 1:]
    target = factor[:, :1]
    coeffs = pl.pallas_call(
        least_squares_kernel,
        out_shape=jax.ShapeDtypeStruct((1, count), jnp.float32),
    )(hessenberg, target)
    return (coeffs[0], thetas)


LANES = 128


def overset_masks(donor_cells, receptor_cells, overset_weight, rows):
    lane_ids = jnp.arange(LANES, dtype=jnp.int32)[:, None]
    row_ids = jnp.arange(rows, dtype=jnp.int32)[:, None]
    donors = donor_cells.reshape(1, -1)
    receptors = receptor_cells.reshape(1, -1)
    weights = overset_weight.reshape(1, -1)
    donor_lane = (donors % LANES == lane_ids).astype(jnp.float32)
    donor_row = (donors // LANES == row_ids).astype(jnp.float32)
    receptor_lane = (receptors % LANES == lane_ids).astype(jnp.float32)
    receptor_row = jnp.where(receptors // LANES == row_ids, weights, 0.0)
    return donor_lane, donor_row, receptor_lane, receptor_row


def loop_roll(values, shift):
    lane_axis = values.ndim - 1
    lanes = lax.broadcasted_iota(jnp.int32, values.shape, lane_axis)
    lane_rolled = jnp.roll(values, shift, axis=lane_axis)
    carried = jnp.roll(lane_rolled, shift, axis=lane_axis - 1)
    edge = 0 if shift > 0 else values.shape[lane_axis] - 1
    return jnp.where(lanes == edge, carried, lane_rolled)


def operate(field, jacobi_inverse, block_couplings, masks):
    donor_lane, donor_row, receptor_lane, receptor_row = masks
    scaled = block_apply(jacobi_inverse, field)
    padded = with_halo(scaled, ((("group", "dev"), 1),), 1)
    result = field + block_apply(block_couplings[0], loop_roll(scaled, 1))
    result = result + block_apply(block_couplings[1], loop_roll(scaled, -1))
    result = result + block_apply(block_couplings[2], padded[:, :-2])
    result = result + block_apply(block_couplings[3], padded[:, 2:])
    comps = scaled.shape[0]
    split_vals = scaled.reshape(comps, -1, LANES)
    partial = jnp.einsum("chl,ls->chs", split_vals, donor_lane, precision=lax.Precision.HIGHEST)
    outgoing = jnp.sum(partial * donor_row[None], axis=1)
    outgoing = outgoing.reshape(comps, lax.axis_size("dev"), -1)
    incoming = lax.all_to_all(outgoing, "dev", split_axis=1, concat_axis=1, tiled=True)
    incoming = incoming.reshape(comps, 1, -1)
    spread = incoming * receptor_row[None]
    moved = jnp.einsum("chs,ls->chl", spread, receptor_lane, precision=lax.Precision.HIGHEST)
    return result - moved.reshape(result.shape)


def layer_onehot(labels, count):
    return (labels[:, None] == jnp.arange(count, dtype=jnp.int32)[None, :]).astype(jnp.float32)


def restrict_field(field, aggregate_map, count):
    totals = jnp.zeros((field.shape[0], count), jnp.float32)
    for k in range(field.shape[1]):
        totals = totals + jnp.dot(
            field[:, k], layer_onehot(aggregate_map[k], count), precision=lax.Precision.HIGHEST
        )
    return totals


def prolong_field(coarse_vals, aggregate_map):
    count = coarse_vals.shape[1]
    layers_out = [
        jnp.dot(
            coarse_vals,
            jnp.transpose(layer_onehot(aggregate_map[k], count)),
            precision=lax.Precision.HIGHEST,
        )
        for k in range(aggregate_map.shape[0])
    ]
    return jnp.stack(layers_out, axis=1)


def body(
    right_side,
    jacobi_inverse,
    block_couplings,
    overset_weight,
    donor_cells,
    receptor_cells,
    aggregate_map,
    coarse_inverse,
    coarse_couplings,
):
    comps, layers, plane = right_side.shape
    tiled = (layers, plane // LANES, LANES)
    masks = overset_masks(donor_cells, receptor_cells, overset_weight, layers * plane // LANES)
    dense_rhs = right_side.reshape((comps,) + tiled)
    dense_inverse = jacobi_inverse.reshape(jacobi_inverse.shape[:2] + tiled)
    dense_couplings = block_couplings.reshape(block_couplings.shape[:3] + tiled)
    krylov = [dense_rhs]
    for j in range(STEPS):
        applied = operate(krylov[j], dense_inverse, dense_couplings, masks)
        krylov.append((applied - shift_value(j, STEPS) * krylov[j]) / BASIS_SCALE)
    stacked = jnp.stack(krylov)
    flat_krylov = [vector.reshape(-1, LANES) for vector in krylov]
    local_gram = pl.pallas_call(
        gram_kernel,
        out_shape=jax.ShapeDtypeStruct((len(krylov), len(krylov)), jnp.float32),
    )(*flat_krylov)
    gram_total = gathered_sum(gathered_sum(local_gram, "dev"), "group")
    coeffs, thetas = small_solve(gram_total)
    combined = jnp.einsum("i,iabcd->abcd", coeffs, stacked[:STEPS], precision=lax.Precision.HIGHEST)
    krylov_update = block_apply(dense_inverse, combined).reshape(right_side.shape)
    applied_combined = sum(
        coeffs[j] * (BASIS_SCALE * krylov[j + 1] + thetas[j] * krylov[j]) for j in range(STEPS)
    )
    new_residual = (dense_rhs - applied_combined).reshape(right_side.shape)
    agg_count = coarse_inverse.shape[2]
    local_rhs = restrict_field(new_residual, aggregate_map, agg_count)
    reach = SWEEPS - 1
    sides = ((("group", "dev"), 1),)
    wide_rhs = with_halo(local_rhs, sides, reach)
    wide_inverse = with_halo(coarse_inverse, ((("group", "dev"), 2),), reach)
    wide_couplings = with_halo(coarse_couplings, ((("group", "dev"), 3),), reach)
    wide_vals = block_apply(wide_inverse, wide_rhs)
    for k in range(SWEEPS - 1):
        zero_col = jnp.zeros_like(wide_vals[:, :1])
        left_vals = jnp.concatenate([zero_col, wide_vals[:, :-1]], axis=1)
        right_vals = jnp.concatenate([wide_vals[:, 1:], zero_col], axis=1)
        wide_vals = block_apply(
            wide_inverse,
            wide_rhs
            - block_apply(wide_couplings[0], left_vals)
            - block_apply(wide_couplings[1], right_vals),
        )
    own_vals = wide_vals[:, reach : wide_vals.shape[1] - reach]
    update = krylov_update + prolong_field(own_vals, aggregate_map)
    return (update, new_residual)


def solution(mesh):
    return jax.shard_map(
        body,
        mesh=mesh,
        in_specs=(
            P(None, ("group", "dev"), None),
            P(None, None, ("group", "dev"), None),
            P(None, None, None, ("group", "dev"), None),
            P(("group", "dev"), None),
            P(("group", "dev"), None),
            P(("group", "dev"), None),
            P(("group", "dev"), None),
            P(None, None, ("group", "dev")),
            P(None, None, None, ("group", "dev")),
        ),
        out_specs=(P(None, ("group", "dev"), None), P(None, ("group", "dev"), None)),
        check_vma=False,
    )
```

```python
import math

import jax
import jax.numpy as jnp
from jax import lax
from jax.experimental import pallas as pl
from jax.sharding import PartitionSpec as P

STEPS = 8
SWEEPS = 4


BASIS_SCALE = 0.5


def with_halo(cells, sides, width):
    for axis, dim in sides:
        count = lax.axis_size(axis)
        ends = count - 1
        head = lax.slice_in_dim(cells, 0, width, axis=dim)
        tail = lax.slice_in_dim(cells, cells.shape[dim] - width, cells.shape[dim], axis=dim)
        cells = jnp.concatenate(
            [
                lax.ppermute(tail, axis, [(i, (i + 1) % count) for i in range(ends)]),
                cells,
                lax.ppermute(head, axis, [((i + 1) % count, i) for i in range(ends)]),
            ],
            axis=dim,
        )
    return cells


def gathered_sum(values, axis):
    count = lax.axis_size(axis)
    copies = jnp.broadcast_to(values[None], (count,) + values.shape)
    return jnp.sum(lax.all_to_all(copies, axis, 0, 0, tiled=True), axis=0)


def block_apply(blocks, vector):
    return jnp.sum(blocks * vector[None], axis=1)


def shift_value(j, count):
    half_index = j // 2
    point = half_index if j % 2 == 0 else count - 1 - half_index
    return 1.0 + 0.5 * math.cos(math.pi * (2 * point + 1) / (2 * count))


def least_squares_kernel(hessenberg_ref, target_ref, coeffs_ref):
    hessenberg = hessenberg_ref[...]
    target = target_ref[...]
    count = hessenberg.shape[1]
    ortho_cols = []
    triangle = {}
    for j in range(count):
        column = hessenberg[:, j : j + 1]
        for i in range(j):
            factor_ij = jnp.sum(ortho_cols[i] * column, axis=0, keepdims=True)
            triangle[i, j] = factor_ij
            column = column - factor_ij * ortho_cols[i]
        length_val = jnp.sqrt(jnp.sum(column * column, axis=0, keepdims=True))
        triangle[j, j] = length_val
        ortho_cols.append(column / length_val)
    projected = [jnp.sum(q * target, axis=0, keepdims=True) for q in ortho_cols]
    solved = [None] * count
    for j in reversed(range(count)):
        running = projected[j]
        for i in range(j + 1, count):
            running = running - triangle[j, i] * solved[i]
        solved[j] = running / triangle[j, j]
    lanes = lax.broadcasted_iota(jnp.int32, (1, count), 1)
    coeffs = jnp.zeros((1, count), jnp.float32)
    for j in range(count):
        coeffs = jnp.where(lanes == j, solved[j], coeffs)
    coeffs_ref[...] = coeffs


def gram_kernel(*refs):
    vector_refs, gram_ref = refs[:-1], refs[-1]
    count = len(vector_refs)
    vectors = [ref[...] for ref in vector_refs]
    rows = lax.broadcasted_iota(jnp.int32, (count, count), 0)
    cols = lax.broadcasted_iota(jnp.int32, (count, count), 1)
    gram = jnp.zeros((count, count), jnp.float32)
    for i in range(count):
        for j in range(i, count):
            product = vectors[i] * vectors[j]
            total = jnp.sum(jnp.sum(product, axis=0, keepdims=True), axis=1, keepdims=True)
            spot = ((rows == i) & (cols == j)) | ((rows == j) & (cols == i))
            gram = jnp.where(spot, total, gram)
    gram_ref[...] = gram


def small_solve(gram_matrix):
    count = gram_matrix.shape[0] - 1
    factor = jnp.transpose(jnp.linalg.cholesky(gram_matrix))
    thetas = jnp.array([shift_value(j, count) for j in range(count)], jnp.float32)
    hessenberg = factor[:, :count] * thetas[None, :] + BASIS_SCALE * factor[:, 1:]
    target = factor[:, :1]
    coeffs = pl.pallas_call(
        least_squares_kernel,
        out_shape=jax.ShapeDtypeStruct((1, count), jnp.float32),
    )(hessenberg, target)
    return (coeffs[0], thetas)


LANES = 128


def overset_masks(donor_cells, receptor_cells, overset_weight, rows):
    lane_ids = jnp.arange(LANES, dtype=jnp.int32)[:, None]
    row_ids = jnp.arange(rows, dtype=jnp.int32)[:, None]
    donors = donor_cells.reshape(1, -1)
    receptors = receptor_cells.reshape(1, -1)
    weights = overset_weight.reshape(1, -1)
    donor_lane = (donors % LANES == lane_ids).astype(jnp.float32)
    donor_row = (donors // LANES == row_ids).astype(jnp.float32)
    receptor_lane = (receptors % LANES == lane_ids).astype(jnp.float32)
    receptor_row = jnp.where(receptors // LANES == row_ids, weights, 0.0)
    return donor_lane, donor_row, receptor_lane, receptor_row


def loop_roll(values, shift):
    lane_axis = values.ndim - 1
    lanes = lax.broadcasted_iota(jnp.int32, values.shape, lane_axis)
    lane_rolled = jnp.roll(values, shift, axis=lane_axis)
    carried = jnp.roll(lane_rolled, shift, axis=lane_axis - 1)
    edge = 0 if shift > 0 else values.shape[lane_axis] - 1
    return jnp.where(lanes == edge, carried, lane_rolled)


def operate(field, jacobi_inverse, block_couplings, masks):
    donor_lane, donor_row, receptor_lane, receptor_row = masks
    scaled = block_apply(jacobi_inverse, field)
    padded = with_halo(scaled, ((("group", "dev"), 1),), 1)
    result = field + block_apply(block_couplings[0], loop_roll(scaled, 1))
    result = result + block_apply(block_couplings[1], loop_roll(scaled, -1))
    result = result + block_apply(block_couplings[2], padded[:, :-2])
    result = result + block_apply(block_couplings[3], padded[:, 2:])
    comps = scaled.shape[0]
    split_vals = scaled.reshape(comps, -1, LANES)
    partial = jnp.einsum("chl,ls->chs", split_vals, donor_lane, precision=lax.Precision.HIGHEST)
    outgoing = jnp.sum(partial * donor_row[None], axis=1)
    outgoing = outgoing.reshape(comps, lax.axis_size("dev"), -1)
    incoming = lax.all_to_all(outgoing, "dev", split_axis=1, concat_axis=1, tiled=True)
    incoming = incoming.reshape(comps, 1, -1)
    spread = incoming * receptor_row[None]
    moved = jnp.einsum("chs,ls->chl", spread, receptor_lane, precision=lax.Precision.HIGHEST)
    return result - moved.reshape(result.shape)


def layer_onehot(labels, count):
    return (labels[:, None] == jnp.arange(count, dtype=jnp.int32)[None, :]).astype(jnp.float32)


def restrict_field(field, aggregate_map, count):
    totals = jnp.zeros((field.shape[0], count), jnp.float32)
    for k in range(field.shape[1]):
        totals = totals + jnp.dot(
            field[:, k], layer_onehot(aggregate_map[k], count), precision=lax.Precision.HIGHEST
        )
    return totals


def prolong_field(coarse_vals, aggregate_map):
    count = coarse_vals.shape[1]
    layers_out = [
        jnp.dot(
            coarse_vals,
            jnp.transpose(layer_onehot(aggregate_map[k], count)),
            precision=lax.Precision.HIGHEST,
        )
        for k in range(aggregate_map.shape[0])
    ]
    return jnp.stack(layers_out, axis=1)


def body(
    right_side,
    jacobi_inverse,
    block_couplings,
    overset_weight,
    donor_cells,
    receptor_cells,
    aggregate_map,
    coarse_inverse,
    coarse_couplings,
):
    comps, layers, plane = right_side.shape
    tiled = (layers, plane // LANES, LANES)
    masks = overset_masks(donor_cells, receptor_cells, overset_weight, layers * plane // LANES)
    dense_rhs = right_side.reshape((comps,) + tiled)
    dense_inverse = jacobi_inverse.reshape(jacobi_inverse.shape[:2] + tiled)
    dense_couplings = block_couplings.reshape(block_couplings.shape[:3] + tiled)
    krylov = [dense_rhs]
    for j in range(STEPS):
        applied = operate(krylov[j], dense_inverse, dense_couplings, masks)
        krylov.append((applied - shift_value(j, STEPS) * krylov[j]) / BASIS_SCALE)
    flat_krylov = [vector.reshape(-1, LANES) for vector in krylov]
    local_gram = pl.pallas_call(
        gram_kernel,
        out_shape=jax.ShapeDtypeStruct((len(krylov), len(krylov)), jnp.float32),
    )(*flat_krylov)
    gram_total = gathered_sum(gathered_sum(local_gram, "dev"), "group")
    coeffs, thetas = small_solve(gram_total)
    combined = sum(coeffs[j] * krylov[j] for j in range(STEPS))
    krylov_update = block_apply(dense_inverse, combined).reshape(right_side.shape)
    applied_combined = sum(
        coeffs[j] * (BASIS_SCALE * krylov[j + 1] + thetas[j] * krylov[j]) for j in range(STEPS)
    )
    new_residual = (dense_rhs - applied_combined).reshape(right_side.shape)
    agg_count = coarse_inverse.shape[2]
    local_rhs = restrict_field(new_residual, aggregate_map, agg_count)
    reach = SWEEPS - 1
    sides = ((("group", "dev"), 1),)
    wide_rhs = with_halo(local_rhs, sides, reach)
    wide_inverse = with_halo(coarse_inverse, ((("group", "dev"), 2),), reach)
    wide_couplings = with_halo(coarse_couplings, ((("group", "dev"), 3),), reach)
    wide_vals = block_apply(wide_inverse, wide_rhs)
    for k in range(SWEEPS - 1):
        zero_col = jnp.zeros_like(wide_vals[:, :1])
        left_vals = jnp.concatenate([zero_col, wide_vals[:, :-1]], axis=1)
        right_vals = jnp.concatenate([wide_vals[:, 1:], zero_col], axis=1)
        wide_vals = block_apply(
            wide_inverse,
            wide_rhs
            - block_apply(wide_couplings[0], left_vals)
            - block_apply(wide_couplings[1], right_vals),
        )
    own_vals = wide_vals[:, reach : wide_vals.shape[1] - reach]
    update = krylov_update + prolong_field(own_vals, aggregate_map)
    return (update, new_residual)


def solution(mesh):
    return jax.shard_map(
        body,
        mesh=mesh,
        in_specs=(
            P(None, ("group", "dev"), None),
            P(None, None, ("group", "dev"), None),
            P(None, None, None, ("group", "dev"), None),
            P(("group", "dev"), None),
            P(("group", "dev"), None),
            P(("group", "dev"), None),
            P(("group", "dev"), None),
            P(None, None, ("group", "dev")),
            P(None, None, None, ("group", "dev")),
        ),
        out_specs=(P(None, ("group", "dev"), None), P(None, ("group", "dev"), None)),
        check_vma=False,
    )
```

```python
import math

import jax
import jax.numpy as jnp
from jax import lax
from jax.experimental import pallas as pl
from jax.sharding import PartitionSpec as P

STEPS = 8
SWEEPS = 4


BASIS_SCALE = 0.5


def with_halo(cells, sides, width):
    for axis, dim in sides:
        count = lax.axis_size(axis)
        ends = count - 1
        head = lax.slice_in_dim(cells, 0, width, axis=dim)
        tail = lax.slice_in_dim(cells, cells.shape[dim] - width, cells.shape[dim], axis=dim)
        cells = jnp.concatenate(
            [
                lax.ppermute(tail, axis, [(i, (i + 1) % count) for i in range(ends)]),
                cells,
                lax.ppermute(head, axis, [((i + 1) % count, i) for i in range(ends)]),
            ],
            axis=dim,
        )
    return cells


def gathered_sum(values, axis):
    count = lax.axis_size(axis)
    copies = jnp.broadcast_to(values[None], (count,) + values.shape)
    return jnp.sum(lax.all_to_all(copies, axis, 0, 0, tiled=True), axis=0)


def block_apply(blocks, vector):
    return jnp.sum(blocks * vector[None], axis=1)


def shift_value(j, count):
    half_index = j // 2
    point = half_index if j % 2 == 0 else count - 1 - half_index
    return 1.0 + 0.5 * math.cos(math.pi * (2 * point + 1) / (2 * count))


def least_squares_kernel(hessenberg_ref, target_ref, coeffs_ref):
    hessenberg = hessenberg_ref[...]
    target = target_ref[...]
    count = hessenberg.shape[1]
    ortho_cols = []
    triangle = {}
    for j in range(count):
        column = hessenberg[:, j : j + 1]
        for i in range(j):
            factor_ij = jnp.sum(ortho_cols[i] * column, axis=0, keepdims=True)
            triangle[i, j] = factor_ij
            column = column - factor_ij * ortho_cols[i]
        length_val = jnp.sqrt(jnp.sum(column * column, axis=0, keepdims=True))
        triangle[j, j] = length_val
        ortho_cols.append(column / length_val)
    projected = [jnp.sum(q * target, axis=0, keepdims=True) for q in ortho_cols]
    solved = [None] * count
    for j in reversed(range(count)):
        running = projected[j]
        for i in range(j + 1, count):
            running = running - triangle[j, i] * solved[i]
        solved[j] = running / triangle[j, j]
    lanes = lax.broadcasted_iota(jnp.int32, (1, count), 1)
    coeffs = jnp.zeros((1, count), jnp.float32)
    for j in range(count):
        coeffs = jnp.where(lanes == j, solved[j], coeffs)
    coeffs_ref[...] = coeffs


def small_solve(gram_matrix):
    count = gram_matrix.shape[0] - 1
    factor = jnp.transpose(jnp.linalg.cholesky(gram_matrix))
    thetas = jnp.array([shift_value(j, count) for j in range(count)], jnp.float32)
    hessenberg = factor[:, :count] * thetas[None, :] + BASIS_SCALE * factor[:, 1:]
    target = factor[:, :1]
    coeffs = pl.pallas_call(
        least_squares_kernel,
        out_shape=jax.ShapeDtypeStruct((1, count), jnp.float32),
    )(hessenberg, target)
    return (coeffs[0], thetas)


LANES = 128


def overset_masks(donor_cells, receptor_cells, overset_weight, rows):
    lane_ids = jnp.arange(LANES, dtype=jnp.int32)[:, None]
    row_ids = jnp.arange(rows, dtype=jnp.int32)[:, None]
    donors = donor_cells.reshape(1, -1)
    receptors = receptor_cells.reshape(1, -1)
    weights = overset_weight.reshape(1, -1)
    donor_lane = (donors % LANES == lane_ids).astype(jnp.float32)
    donor_row = (donors // LANES == row_ids).astype(jnp.float32)
    receptor_lane = (receptors % LANES == lane_ids).astype(jnp.float32)
    receptor_row = jnp.where(receptors // LANES == row_ids, weights, 0.0)
    return donor_lane, donor_row, receptor_lane, receptor_row


def loop_roll(values, shift):
    lane_axis = values.ndim - 1
    lanes = lax.broadcasted_iota(jnp.int32, values.shape, lane_axis)
    lane_rolled = jnp.roll(values, shift, axis=lane_axis)
    carried = jnp.roll(lane_rolled, shift, axis=lane_axis - 1)
    edge = 0 if shift > 0 else values.shape[lane_axis] - 1
    return jnp.where(lanes == edge, carried, lane_rolled)


def operate(field, jacobi_inverse, block_couplings, masks):
    donor_lane, donor_row, receptor_lane, receptor_row = masks
    scaled = block_apply(jacobi_inverse, field)
    padded = with_halo(scaled, ((("group", "dev"), 1),), 1)
    result = field + block_apply(block_couplings[0], loop_roll(scaled, 1))
    result = result + block_apply(block_couplings[1], loop_roll(scaled, -1))
    result = result + block_apply(block_couplings[2], padded[:, :-2])
    result = result + block_apply(block_couplings[3], padded[:, 2:])
    comps = scaled.shape[0]
    split_vals = scaled.reshape(comps, -1, LANES)
    partial = jnp.einsum("chl,ls->chs", split_vals, donor_lane, precision=lax.Precision.HIGHEST)
    outgoing = jnp.sum(partial * donor_row[None], axis=1)
    outgoing = outgoing.reshape(comps, lax.axis_size("dev"), -1)
    incoming = lax.all_to_all(outgoing, "dev", split_axis=1, concat_axis=1, tiled=True)
    incoming = incoming.reshape(comps, 1, -1)
    spread = incoming * receptor_row[None]
    moved = jnp.einsum("chs,ls->chl", spread, receptor_lane, precision=lax.Precision.HIGHEST)
    return result - moved.reshape(result.shape)


def layer_onehot(labels, count):
    return (labels[:, None] == jnp.arange(count, dtype=jnp.int32)[None, :]).astype(jnp.float32)


def restrict_field(field, aggregate_map, count):
    totals = jnp.zeros((field.shape[0], count), jnp.float32)
    for k in range(field.shape[1]):
        totals = totals + jnp.dot(
            field[:, k], layer_onehot(aggregate_map[k], count), precision=lax.Precision.HIGHEST
        )
    return totals


def prolong_field(coarse_vals, aggregate_map):
    count = coarse_vals.shape[1]
    layers_out = [
        jnp.dot(
            coarse_vals,
            jnp.transpose(layer_onehot(aggregate_map[k], count)),
            precision=lax.Precision.HIGHEST,
        )
        for k in range(aggregate_map.shape[0])
    ]
    return jnp.stack(layers_out, axis=1)


def body(
    right_side,
    jacobi_inverse,
    block_couplings,
    overset_weight,
    donor_cells,
    receptor_cells,
    aggregate_map,
    coarse_inverse,
    coarse_couplings,
):
    comps, layers, plane = right_side.shape
    tiled = (layers, plane // LANES, LANES)
    masks = overset_masks(donor_cells, receptor_cells, overset_weight, layers * plane // LANES)
    dense_rhs = right_side.reshape((comps,) + tiled)
    dense_inverse = jacobi_inverse.reshape(jacobi_inverse.shape[:2] + tiled)
    dense_couplings = block_couplings.reshape(block_couplings.shape[:3] + tiled)
    krylov = [dense_rhs]
    for j in range(STEPS):
        applied = operate(krylov[j], dense_inverse, dense_couplings, masks)
        krylov.append((applied - shift_value(j, STEPS) * krylov[j]) / BASIS_SCALE)
    stacked = jnp.stack(krylov)
    local_gram = jnp.einsum("iabcd,jabcd->ij", stacked, stacked, precision=lax.Precision.HIGHEST)
    gram_total = gathered_sum(gathered_sum(local_gram, "dev"), "group")
    coeffs, thetas = small_solve(gram_total)
    combined = jnp.einsum("i,iabcd->abcd", coeffs, stacked[:STEPS], precision=lax.Precision.HIGHEST)
    krylov_update = block_apply(dense_inverse, combined).reshape(right_side.shape)
    applied_combined = sum(
        coeffs[j] * (BASIS_SCALE * krylov[j + 1] + thetas[j] * krylov[j]) for j in range(STEPS)
    )
    new_residual = (dense_rhs - applied_combined).reshape(right_side.shape)
    agg_count = coarse_inverse.shape[2]
    local_rhs = restrict_field(new_residual, aggregate_map, agg_count)
    reach = SWEEPS - 1
    sides = ((("group", "dev"), 1),)
    wide_rhs = with_halo(local_rhs, sides, reach)
    coarse_blocks = jnp.concatenate([coarse_inverse[None], coarse_couplings], axis=0)
    wide_blocks = with_halo(coarse_blocks, ((("group", "dev"), 3),), reach)
    wide_inverse = wide_blocks[0]
    wide_couplings = wide_blocks[1:]
    wide_vals = block_apply(wide_inverse, wide_rhs)
    for k in range(SWEEPS - 1):
        zero_col = jnp.zeros_like(wide_vals[:, :1])
        left_vals = jnp.concatenate([zero_col, wide_vals[:, :-1]], axis=1)
        right_vals = jnp.concatenate([wide_vals[:, 1:], zero_col], axis=1)
        wide_vals = block_apply(
            wide_inverse,
            wide_rhs
            - block_apply(wide_couplings[0], left_vals)
            - block_apply(wide_couplings[1], right_vals),
        )
    own_vals = wide_vals[:, reach : wide_vals.shape[1] - reach]
    update = krylov_update + prolong_field(own_vals, aggregate_map)
    return (update, new_residual)


def solution(mesh):
    return jax.shard_map(
        body,
        mesh=mesh,
        in_specs=(
            P(None, ("group", "dev"), None),
            P(None, None, ("group", "dev"), None),
            P(None, None, None, ("group", "dev"), None),
            P(("group", "dev"), None),
            P(("group", "dev"), None),
            P(("group", "dev"), None),
            P(("group", "dev"), None),
            P(None, None, ("group", "dev")),
            P(None, None, None, ("group", "dev")),
        ),
        out_specs=(P(None, ("group", "dev"), None), P(None, ("group", "dev"), None)),
        check_vma=False,
    )
```
